32 devices in a mesh: dp: 2 (over x), ctx: 16 (over z, y, core).
Axes of the slice: x: 2, y: 2, z: 4, core: 2. Of those that a mesh axis runs over, the one named last changes fastest.
Arguments:
- queries: bfloat16 [4096, 4096], P(('dp', 'ctx')), parts along dimension 0, may hold values from -6 to 6
- keys: bfloat16 [4096, 4096], P(('dp', 'ctx')), parts along dimension 0, may hold values from -6 to 6
- values: bfloat16 [4096, 4096], P(('dp', 'ctx')), parts along dimension 0, may hold values from -6 to 6
- taps: bfloat16 [512, 256], P('ctx'), may hold values from -0.25 to 0.25
- segment_ids: int32 [4096], P(('dp', 'ctx')), parts along dimension 0, may hold values from 0 to 3, never falling along the last dimension, each value on 1 to 1024 neighbouring positions
Outputs:
- mixed: bfloat16 [4096, 4096], P(('dp', 'ctx')), parts along dimension 0
The draws below stay inside these ranges and needn't reach their ends.
There are 2 independent parts, one for each index of `dp`. The reference program is written for one: setup_inputs(seed, part) draws one part's arguments, and reference() takes and returns one part's arrays. A program takes and returns all parts, laid end to end along the dimension named above; an argument that names none is the same for every part. Nothing has to cross between parts.
Inputs may be any that keep to these rules, and one draw needn't show every extreme that they name: `segment_ids`: ids never fall along the sequence; every id from 0 to 3 appears; each document holds 1 to 1024 positions and one holds exactly 1024.
All inputs are finite; a program needn't handle non-finite values.
Results may differ from the reference program's by a relative error of at most 0.0056.
Values may be sent and summed in bfloat16 or wider, within the bound.
No kernel may reach another device: no remote copies, remote signals or barrier semaphores. Data moves between devices by JAX's collectives and lax.ppermute only.
A program may use at most 128 MiB of HBM per device.

```python
import math
import jax
import jax.numpy as jnp
import numpy as np
from jax import lax

D = 4096
GROUP = 16
FILTERS = 256
T_DEV = 128
LAGS = 4
FILT_LEN = 512
SEQ = 2048
DOCS = 4
N_CTX = 16


def levels(own_key, dims, split, smallest, top_value):
    loudness = 1.0
    for axis_at, parts in split:
        heights = jax.random.uniform(jax.random.fold_in(jax.random.fold_in(own_key, 6), axis_at), (parts,), jnp.float32, smallest / len(split), top_value / len(split))
        loudness = loudness * jnp.repeat(jnp.exp(heights), dims[axis_at] // parts).reshape((-1,) + (1,) * (len(dims) - 1 - axis_at))
    return loudness


def split_up(count, total, most, slope):
    loads = [(1 << 20) // math.isqrt(standing ** slope) + 1 for standing in range(2, count + 1)]
    surplus, given = total - most - (count - 1), [1] * (count - 1)
    while surplus > 0:
        movable = [i for i in range(count - 1) if given[i] < most]
        pool, remaining = sum([loads[i] for i in movable]), surplus
        for i in movable:
            more = min(most - given[i], max(1, remaining * loads[i] // pool), surplus)
            given[i] = given[i] + more
            surplus = surplus - more
    return np.array([most] + given)


def uneven(stream_key, amount, total, reach, skew):
    if amount == 2:
        one = jax.random.randint(stream_key, (), max(1, total - reach), min(reach, total - 1) + 1)
        return jnp.stack([one, total - one])
    sizes = jnp.asarray(split_up(amount, total, reach, skew), jnp.int32)
    pairs = (amount - 1) // 2
    source_of, receiver = sizes[1:1 + 2 * pairs:2], sizes[2:2 + 2 * pairs:2]
    slack = jnp.minimum(source_of - 1, reach - receiver)
    shifted = jax.random.randint(jax.random.fold_in(stream_key, 1), (pairs,), 0, 1 << 20) % (slack + 1)
    sizes = sizes.at[1:1 + 2 * pairs:2].set(source_of - shifted).at[2:2 + 2 * pairs:2].set(receiver + shifted)
    return sizes[jax.random.permutation(jax.random.fold_in(stream_key, 2), amount)]


def normal_values(own_key, shape, spread, most, pieces=(), kind=jnp.bfloat16):
    loudness = levels(own_key, shape, pieces, -0.22, 0.18) if pieces else 1.0
    entries = jax.random.normal(own_key, shape, jnp.float32) * spread * loudness
    return jnp.minimum(jnp.maximum(entries, -most), most).astype(kind)


def setup_inputs(seed: int = 0, part: int = 0) -> dict:
    key_of = jax.random.split(jax.random.key(seed), 6)
    part_keys = jax.random.split(jax.random.fold_in(key_of[5], part), 6)
    queries = normal_values(part_keys[0], (SEQ, D), 1.0, 6.0, ((0, 16),))
    keys = normal_values(part_keys[1], (SEQ, D), 1.0, 6.0, ((0, 16),))
    values = normal_values(part_keys[2], (SEQ, D), 1.0, 6.0, ((0, 16),))
    taps = normal_values(key_of[3], (FILT_LEN, FILTERS), FILT_LEN ** -0.5, 0.25, ((0, 16),))
    segment_ids = jnp.searchsorted(jnp.cumsum(uneven(part_keys[4], DOCS, SEQ, SEQ // 2, 2)), jnp.arange(SEQ), side="right").astype(jnp.int32)
    return dict(queries=queries, keys=keys, values=values, taps=taps, segment_ids=segment_ids)


def pair_term(padded_taps, lag_blocks, seg_target, seg_source, source_rows):
    out_pos = jnp.arange(T_DEV, dtype=jnp.int32)[:, None]
    in_pos = jnp.arange(T_DEV, dtype=jnp.int32)[None, :]
    tap_index = (lag_blocks * T_DEV + out_pos - in_pos).astype(jnp.int32)
    allowed = (tap_index >= 0) & (tap_index < FILT_LEN) & (seg_target[:, None] == seg_source[None, :])
    tiled = padded_taps[tap_index + T_DEV]
    weights = jnp.where(allowed[:, :, None], tiled.astype(jnp.float32), 0.0)
    shaped = source_rows.astype(jnp.float32).reshape(T_DEV, FILTERS, GROUP)
    return jnp.einsum('tsf,sfg->tfg', weights, shaped).reshape(T_DEV, D)


def reference(queries, keys, values, taps, segment_ids):
    gated = (keys.astype(jnp.float32) * values.astype(jnp.float32)).astype(jnp.bfloat16)
    zero_rows = jnp.zeros((T_DEV, FILTERS), jnp.bfloat16)
    padded_taps = jnp.concatenate([zero_rows, taps, zero_rows], axis=0)
    gated_blocks = gated.reshape(N_CTX, T_DEV, D)
    seg_blocks = segment_ids.reshape(N_CTX, T_DEV)
    query_blocks = queries.reshape(N_CTX, T_DEV, D)

    def out_block(target):
        seg_target = lax.dynamic_index_in_dim(seg_blocks, target, 0, keepdims=False)
        own_rows = lax.dynamic_index_in_dim(gated_blocks, target, 0, keepdims=False)
        own_term = pair_term(padded_taps, jnp.int32(0), seg_target, seg_target, own_rows)

        def add_source(source, summed):
            seg_source = lax.dynamic_index_in_dim(seg_blocks, source, 0, keepdims=False)
            source_rows = lax.dynamic_index_in_dim(gated_blocks, source, 0, keepdims=False)
            term = pair_term(padded_taps, (target - source).astype(jnp.int32), seg_target, seg_source, source_rows)
            rounded = lax.optimization_barrier(term.astype(jnp.bfloat16))
            return summed + rounded.astype(jnp.float32)

        first = jnp.maximum(target - LAGS, 0).astype(jnp.int32)
        summed = lax.fori_loop(first, target, add_source, own_term)
        query_rows = lax.dynamic_index_in_dim(query_blocks, target, 0, keepdims=False)
        return (query_rows.astype(jnp.float32) * summed).astype(jnp.bfloat16)

    mixed = lax.map(out_block, jnp.arange(N_CTX, dtype=jnp.int32))
    return mixed.reshape(SEQ, D)
```

```python
import functools

import jax
import jax.numpy as jnp
from jax import lax
from jax.experimental import pallas as pl
from jax.experimental.pallas import tpu as pltpu
from jax.sharding import PartitionSpec as P


def shifted(value, axis, steps):
    count = lax.axis_size(axis)
    first, last = (max(0, -steps), min(count, count - steps))
    return lax.ppermute(value, axis, [(source, source + steps) for source in range(first, last)])


def conv_kernel(*refs, lags, rows, group_size, lane_chunk):
    g_refs = refs[:lags + 1]
    p_ref, m_ref, q_ref, o_ref, lhs_ref, rhs_ref = refs[lags + 1:]
    per_chunk = lane_chunk // group_size
    row = lax.broadcasted_iota(jnp.int32, (rows, rows), 0)
    upper = lax.broadcasted_iota(jnp.int32, (rows, rows), 1) >= row
    owner = lax.broadcasted_iota(jnp.int32, (rows, lane_chunk), 1) // group_size
    for k in range(per_chunk):
        tap_row = p_ref[k : k + 1, :]
        rolled = [
            pltpu.roll(
                jnp.broadcast_to(tap_row[:, rows * m : rows * (m + 1)], (rows, rows)),
                0,
                1,
                stride=1,
                stride_axis=0,
            )
            for m in range(lags + 2)
        ]
        for n in range(lags + 1):
            tile = jnp.where(upper, rolled[n + 1], rolled[n]) * m_ref[:, rows * n : rows * (n + 1)]
            lhs_ref[n, :, rows * k : rows * (k + 1)] = tile.astype(jnp.bfloat16)
    acc = jnp.zeros((rows, lane_chunk), jnp.float32)
    for n in range(lags + 1):
        source = g_refs[n][...]
        for k in range(per_chunk):
            rhs_ref[rows * k : rows * (k + 1), :] = jnp.where(owner == k, source, jnp.zeros_like(source))
        term = jnp.dot(lhs_ref[n], rhs_ref[...], preferred_element_type=jnp.float32)
        if n < lags:
            term = term.astype(jnp.bfloat16).astype(jnp.float32)
        acc = acc + term
    o_ref[...] = (q_ref[...].astype(jnp.float32) * acc).astype(o_ref.dtype)


def shards(queries, keys, values, taps, segment_ids):
    rows = queries.shape[0]
    channels = queries.shape[1]
    filters = taps.shape[1]
    group_size = channels // filters
    gated = (keys.astype(jnp.float32) * values.astype(jnp.float32)).astype(jnp.bfloat16)
    all_taps = lax.all_gather(taps, "ctx", axis=0, tiled=True)
    filt_len = all_taps.shape[0]
    lags = filt_len // rows
    padded = jnp.concatenate(
        [
            jnp.zeros((filters, rows + 1), jnp.float32),
            all_taps.T[:, ::-1].astype(jnp.float32),
            jnp.zeros((filters, rows - 1), jnp.float32),
        ],
        axis=1,
    )
    sources = [shifted(gated, "ctx", lag) for lag in range(lags, 0, -1)] + [gated]
    seg_sources = [shifted(segment_ids, "ctx", lag) for lag in range(lags, 0, -1)]
    seg_all = jnp.concatenate(seg_sources + [segment_ids])
    mask = (segment_ids[:, None] == seg_all[None, :]).astype(jnp.float32)
    lane_chunk = 128
    filt_per_chunk = lane_chunk // group_size
    span = (lags + 1) * rows
    kernel = functools.partial(
        conv_kernel, lags=lags, rows=rows, group_size=group_size, lane_chunk=lane_chunk
    )
    block = pl.BlockSpec((rows, lane_chunk), lambda j: (0, j))
    return pl.pallas_call(
        kernel,
        grid=(channels // lane_chunk,),
        in_specs=[block] * (lags + 1)
        + [
            pl.BlockSpec((filt_per_chunk, (lags + 2) * rows), lambda j: (j, 0)),
            pl.BlockSpec((rows, span), lambda j: (0, 0)),
            block,
        ],
        out_specs=block,
        out_shape=jax.ShapeDtypeStruct((rows, channels), jnp.bfloat16),
        scratch_shapes=[
            pltpu.VMEM((lags + 1, rows, rows * filt_per_chunk), jnp.bfloat16),
            pltpu.VMEM((rows * filt_per_chunk, lane_chunk), jnp.bfloat16),
        ],
    )(*sources, padded, mask, queries)


def solution(mesh):
    return jax.shard_map(
        shards,
        mesh=mesh,
        in_specs=(
            P(("dp", "ctx"), None),
            P(("dp", "ctx"), None),
            P(("dp", "ctx"), None),
            P("ctx", None),
            P(("dp", "ctx")),
        ),
        out_specs=P(("dp", "ctx"), None),
        check_vma=False,
    )
```

```python
import functools

import jax
import jax.numpy as jnp
from jax import lax
from jax.experimental import pallas as pl
from jax.experimental.pallas import tpu as pltpu
from jax.sharding import PartitionSpec as P


def shifted(value, axis, steps):
    count = lax.axis_size(axis)
    first, last = (max(0, -steps), min(count, count - steps))
    return lax.ppermute(value, axis, [(source, source + steps) for source in range(first, last)])


def swapped(value, axis):
    count = lax.axis_size(axis)
    return lax.ppermute(value, axis, [(source, source ^ 1) for source in range(count)])


def lag_kernel(tile_ref, g_ref, lo_ref, hi_ref, m_ref, *rest, rows, group_size, first, final, rounded):
    rest = list(rest)
    acc_ref = None if first else rest.pop(0)
    q_ref = rest.pop(0) if final else None
    o_ref, lhs_ref, rhs_ref = rest
    lane_chunk = g_ref.shape[1]
    row = lax.broadcasted_iota(jnp.int32, (rows, rows), 0)
    upper = lax.broadcasted_iota(jnp.int32, (rows, rows), 1) >= row
    owner = lax.broadcasted_iota(jnp.int32, (rows, lane_chunk), 1) // group_size
    source = g_ref[...]
    mask = m_ref[...]
    for k in range(lane_chunk // group_size):
        lo = pltpu.roll(jnp.broadcast_to(lo_ref[k : k + 1, :], (rows, rows)), 0, 1, stride=1, stride_axis=0)
        hi = pltpu.roll(jnp.broadcast_to(hi_ref[k : k + 1, :], (rows, rows)), 0, 1, stride=1, stride_axis=0)
        lhs_ref[:, rows * k : rows * (k + 1)] = (jnp.where(upper, hi, lo) * mask).astype(jnp.bfloat16)
        rhs_ref[rows * k : rows * (k + 1), :] = jnp.where(owner == k, source, jnp.zeros_like(source))
    term = jnp.dot(lhs_ref[...], rhs_ref[...], preferred_element_type=jnp.float32)
    if rounded:
        term = term.astype(jnp.bfloat16).astype(jnp.float32)
    if acc_ref is not None:
        term = acc_ref[...] + term
    if final:
        o_ref[...] = (q_ref[...].astype(jnp.float32) * term).astype(o_ref.dtype)
    else:
        o_ref[...] = term


def lag_term(tile, source, padded, mask, acc, queries, *, group_size, rounded, final):
    rows, channels = source.shape
    lane_chunk = 128
    per_chunk = lane_chunk // group_size
    first = acc is None
    block = pl.BlockSpec((rows, lane_chunk), lambda j, t: (0, j))
    in_specs = [
        block,
        pl.BlockSpec((per_chunk, rows), lambda j, t: (j, t[0])),
        pl.BlockSpec((per_chunk, rows), lambda j, t: (j, t[0] + 1)),
        pl.BlockSpec((rows, rows), lambda j, t: (0, 0)),
    ]
    operands = [source, padded, padded, mask]
    if not first:
        in_specs.append(block)
        operands.append(acc)
    if final:
        in_specs.append(block)
        operands.append(queries)
    kernel = functools.partial(
        lag_kernel, rows=rows, group_size=group_size, first=first, final=final, rounded=rounded
    )
    out_dtype = queries.dtype if final else jnp.float32
    return pl.pallas_call(
        kernel,
        grid_spec=pltpu.PrefetchScalarGridSpec(
            num_scalar_prefetch=1,
            grid=(channels // lane_chunk,),
            in_specs=in_specs,
            out_specs=block,
            scratch_shapes=[
                pltpu.VMEM((rows, rows * per_chunk), jnp.bfloat16),
                pltpu.VMEM((rows * per_chunk, lane_chunk), jnp.bfloat16),
            ],
        ),
        out_shape=jax.ShapeDtypeStruct((rows, channels), out_dtype),
    )(jnp.reshape(tile, (1,)).astype(jnp.int32), *operands)


def shards(queries, keys, values, taps, segment_ids):
    rows = queries.shape[0]
    channels = queries.shape[1]
    filters = taps.shape[1]
    group_size = channels // filters
    own_index = lax.axis_index("ctx")
    core = own_index % 2
    all_taps = lax.all_gather(taps, "ctx", axis=0, tiled=True)
    all_segs = lax.all_gather(segment_ids, "ctx", axis=0, tiled=True)
    gated = (keys.astype(jnp.float32) * values.astype(jnp.float32)).astype(jnp.bfloat16)
    all_taps, all_segs, gated = lax.optimization_barrier((all_taps, all_segs, gated))
    filt_len = all_taps.shape[0]
    lags = filt_len // rows
    padded = jnp.concatenate(
        [
            jnp.zeros((filters, rows + 1), jnp.float32),
            all_taps.T[:, ::-1].astype(jnp.float32),
            jnp.zeros((filters, rows - 1), jnp.float32),
        ],
        axis=1,
    )

    def mask_for(lag):
        start = jnp.maximum(own_index - lag, 0) * rows
        seg_source = lax.dynamic_slice_in_dim(all_segs, start, rows)
        return (segment_ids[:, None] == seg_source[None, :]).astype(jnp.float32)

    two_back = shifted(gated, "ctx", 2)
    four_back = shifted(gated, "ctx", 4)
    swap_a = swapped(two_back, "ctx")
    swap_b = swapped(jnp.where(core == 1, four_back, gated), "ctx")
    lag_a = 1 + 2 * core
    lag_b = 3 - 2 * core
    step = functools.partial(lag_term, padded=padded, queries=queries, group_size=group_size)
    acc = step(jnp.int32(lags), gated, mask=mask_for(0), acc=None, rounded=False, final=False)
    acc = step(jnp.int32(lags - 2), two_back, mask=mask_for(2), acc=acc, rounded=True, final=False)
    acc = step(lags - lag_a, swap_a, mask=mask_for(lag_a), acc=acc, rounded=True, final=False)
    acc = step(jnp.int32(lags - 4), four_back, mask=mask_for(4), acc=acc, rounded=True, final=False)
    return step(lags - lag_b, swap_b, mask=mask_for(lag_b), acc=acc, rounded=True, final=True)


def solution(mesh):
    return jax.shard_map(
        shards,
        mesh=mesh,
        in_specs=(
            P(("dp", "ctx"), None),
            P(("dp", "ctx"), None),
            P(("dp", "ctx"), None),
            P("ctx", None),
            P(("dp", "ctx")),
        ),
        out_specs=P(("dp", "ctx"), None),
        check_vma=False,
    )
```

```python
import functools

import jax
import jax.numpy as jnp
from jax import lax
from jax.experimental import pallas as pl
from jax.experimental.pallas import tpu as pltpu
from jax.sharding import PartitionSpec as P


def shifted(value, axis, steps):
    count = lax.axis_size(axis)
    first, last = (max(0, -steps), min(count, count - steps))
    return lax.ppermute(value, axis, [(source, source + steps) for source in range(first, last)])


def swapped(value, axis):
    count = lax.axis_size(axis)
    return lax.ppermute(value, axis, [(source, source ^ 1) for source in range(count)])


def conv_kernel(core_ref, *refs, lags, rows, group_size):
    g_refs = list(refs[:lags + 1])
    p_ref, m_ref, q_ref, o_ref, lhs_ref, rhs_ref = refs[lags + 1:]
    lane_chunk = q_ref.shape[1]
    per_chunk = lane_chunk // group_size
    row = lax.broadcasted_iota(jnp.int32, (rows, rows), 0)
    upper = lax.broadcasted_iota(jnp.int32, (rows, rows), 1) >= row
    owner = lax.broadcasted_iota(jnp.int32, (rows, lane_chunk), 1) // group_size
    for k in range(per_chunk):
        tap_row = p_ref[k : k + 1, :]
        rolled = [
            pltpu.roll(
                jnp.broadcast_to(tap_row[:, rows * m : rows * (m + 1)], (rows, rows)),
                0,
                1,
                stride=1,
                stride_axis=0,
            )
            for m in range(lags + 2)
        ]
        for n in range(lags + 1):
            tile = jnp.where(upper, rolled[n + 1], rolled[n]) * m_ref[:, rows * n : rows * (n + 1)]
            lhs_ref[n, :, rows * k : rows * (k + 1)] = tile.astype(jnp.bfloat16)
    even = core_ref[0] == 0
    near, far = g_refs[lags - 1][...], g_refs[lags - 3][...]
    blocks = [g[...] for g in g_refs]
    blocks[lags - 1] = jnp.where(even, near, far)
    blocks[lags - 3] = jnp.where(even, far, near)
    acc = jnp.zeros((rows, lane_chunk), jnp.float32)
    for n in range(lags + 1):
        source = blocks[n]
        for k in range(per_chunk):
            rhs_ref[rows * k : rows * (k + 1), :] = jnp.where(owner == k, source, jnp.zeros_like(source))
        term = jnp.dot(lhs_ref[n], rhs_ref[...], preferred_element_type=jnp.float32)
        if n < lags:
            term = term.astype(jnp.bfloat16).astype(jnp.float32)
        acc = acc + term
    o_ref[...] = (q_ref[...].astype(jnp.float32) * acc).astype(o_ref.dtype)


def shards(queries, keys, values, taps, segment_ids):
    rows = queries.shape[0]
    channels = queries.shape[1]
    filters = taps.shape[1]
    group_size = channels // filters
    ctx_count = lax.axis_size("ctx")
    own_index = lax.axis_index("ctx")
    core = own_index % 2
    tap_rows = taps.shape[0]
    filt_len = tap_rows * ctx_count
    lags = filt_len // rows
    packed = jnp.zeros((filt_len + ctx_count, filters), jnp.float32)
    packed = lax.dynamic_update_slice(packed, taps.astype(jnp.float32), (own_index * tap_rows, 0))
    seg_row = jnp.zeros((1, filters), jnp.float32).at[0, :rows].set(segment_ids.astype(jnp.float32))
    packed = lax.dynamic_update_slice(packed, seg_row, (filt_len + own_index, 0))
    packed = lax.psum(packed, "ctx")
    all_taps = packed[:filt_len]
    all_segs = packed[filt_len:, :rows].astype(jnp.int32)
    gated = (keys.astype(jnp.float32) * values.astype(jnp.float32)).astype(jnp.bfloat16)
    padded = jnp.concatenate(
        [
            jnp.zeros((filters, rows + 1), jnp.float32),
            all_taps.T[:, ::-1],
            jnp.zeros((filters, rows - 1), jnp.float32),
        ],
        axis=1,
    )
    seg_sources = [
        lax.dynamic_index_in_dim(all_segs, jnp.maximum(own_index - lag, 0), 0, keepdims=False)
        for lag in range(lags, -1, -1)
    ]
    mask = (segment_ids[:, None] == jnp.concatenate(seg_sources)[None, :]).astype(jnp.float32)
    two_back = shifted(gated, "ctx", 2)
    four_back = shifted(gated, "ctx", 4)
    swap_a = swapped(two_back, "ctx")
    swap_b = swapped(jnp.where(core == 1, four_back, gated), "ctx")
    sources = [four_back, swap_b, two_back, swap_a, gated]
    lane_chunk = 128
    per_chunk = lane_chunk // group_size
    span = (lags + 1) * rows
    kernel = functools.partial(conv_kernel, lags=lags, rows=rows, group_size=group_size)
    block = pl.BlockSpec((rows, lane_chunk), lambda j, c: (0, j))
    return pl.pallas_call(
        kernel,
        grid_spec=pltpu.PrefetchScalarGridSpec(
            num_scalar_prefetch=1,
            grid=(channels // lane_chunk,),
            in_specs=[block] * (lags + 1)
            + [
                pl.BlockSpec((per_chunk, (lags + 2) * rows), lambda j, c: (j, 0)),
                pl.BlockSpec((rows, span), lambda j, c: (0, 0)),
                block,
            ],
            out_specs=block,
            scratch_shapes=[
                pltpu.VMEM((lags + 1, rows, rows * per_chunk), jnp.bfloat16),
                pltpu.VMEM((rows * per_chunk, lane_chunk), jnp.bfloat16),
            ],
        ),
        out_shape=jax.ShapeDtypeStruct((rows, channels), jnp.bfloat16),
    )(jnp.reshape(core, (1,)).astype(jnp.int32), *sources, padded, mask, queries)


def solution(mesh):
    return jax.shard_map(
        shards,
        mesh=mesh,
        in_specs=(
            P(("dp", "ctx"), None),
            P(("dp", "ctx"), None),
            P(("dp", "ctx"), None),
            P("ctx", None),
            P(("dp", "ctx")),
        ),
        out_specs=P(("dp", "ctx"), None),
        check_vma=False,
    )
```

```python
import functools

import jax
import jax.numpy as jnp
from jax import lax
from jax.experimental import pallas as pl
from jax.experimental.pallas import tpu as pltpu
from jax.sharding import PartitionSpec as P


def shifted(value, axis, steps):
    count = lax.axis_size(axis)
    first, last = (max(0, -steps), min(count, count - steps))
    return lax.ppermute(value, axis, [(source, source + steps) for source in range(first, last)])


def swapped(value, axis):
    count = lax.axis_size(axis)
    return lax.ppermute(value, axis, [(source, source ^ 1) for source in range(count)])


def conv_kernel(core_ref, *refs, lags, rows, group_size):
    g_refs = list(refs[:lags + 1])
    p_ref, m_ref, q_ref, o_ref, lhs_ref, rhs_ref = refs[lags + 1:]
    lane_chunk = q_ref.shape[1]
    per_chunk = lane_chunk // group_size
    row = lax.broadcasted_iota(jnp.int32, (rows, rows), 0)
    upper = lax.broadcasted_iota(jnp.int32, (rows, rows), 1) >= row
    owner = lax.broadcasted_iota(jnp.int32, (rows, lane_chunk), 1) // group_size
    for k in range(per_chunk):
        tap_row = p_ref[k : k + 1, :]
        rolled = [
            pltpu.roll(
                jnp.broadcast_to(tap_row[:, rows * m : rows * (m + 1)], (rows, rows)),
                0,
                1,
                stride=1,
                stride_axis=0,
            )
            for m in range(lags + 2)
        ]
        for n in range(lags + 1):
            tile = jnp.where(upper, rolled[n + 1], rolled[n]) * m_ref[:, rows * n : rows * (n + 1)]
            lhs_ref[n, :, rows * k : rows * (k + 1)] = tile.astype(jnp.bfloat16)
    even = core_ref[0] == 0
    near, far = g_refs[lags - 1][...], g_refs[lags - 3][...]
    blocks = [g[...] for g in g_refs]
    blocks[lags - 1] = jnp.where(even, near, far)
    blocks[lags - 3] = jnp.where(even, far, near)
    acc = jnp.zeros((rows, lane_chunk), jnp.float32)
    for n in range(lags + 1):
        source = blocks[n]
        for k in range(per_chunk):
            rhs_ref[rows * k : rows * (k + 1), :] = jnp.where(owner == k, source, jnp.zeros_like(source))
        term = jnp.dot(lhs_ref[n], rhs_ref[...], preferred_element_type=jnp.float32)
        if n < lags:
            term = term.astype(jnp.bfloat16).astype(jnp.float32)
        acc = acc + term
    o_ref[...] = (q_ref[...].astype(jnp.float32) * acc).astype(o_ref.dtype)


def shards(queries, keys, values, taps, segment_ids):
    rows = queries.shape[0]
    channels = queries.shape[1]
    filters = taps.shape[1]
    group_size = channels // filters
    ctx_count = lax.axis_size("ctx")
    own_index = lax.axis_index("ctx")
    core = own_index % 2
    tap_rows = taps.shape[0]
    filt_len = tap_rows * ctx_count
    lags = filt_len // rows
    seg_row = jnp.zeros((1, filters), jnp.float32).at[0, :rows].set(segment_ids.astype(jnp.float32))
    packed = jnp.concatenate([taps.astype(jnp.float32), seg_row], axis=0)
    packed = lax.all_gather(packed, "ctx", axis=0, tiled=False)
    packed, keys, values = lax.optimization_barrier((packed, keys, values))
    all_taps = packed[:, :tap_rows].reshape(filt_len, filters)
    all_segs = packed[:, tap_rows, :rows].astype(jnp.int32)
    gated = (keys.astype(jnp.float32) * values.astype(jnp.float32)).astype(jnp.bfloat16)
    padded = jnp.concatenate(
        [
            jnp.zeros((filters, rows + 1), jnp.float32),
            all_taps.T[:, ::-1],
            jnp.zeros((filters, rows - 1), jnp.float32),
        ],
        axis=1,
    )
    seg_sources = [
        lax.dynamic_index_in_dim(all_segs, jnp.maximum(own_index - lag, 0), 0, keepdims=False)
        for lag in range(lags, -1, -1)
    ]
    mask = (segment_ids[:, None] == jnp.concatenate(seg_sources)[None, :]).astype(jnp.float32)
    two_back = shifted(gated, "ctx", 2)
    four_back = shifted(gated, "ctx", 4)
    swap_a = swapped(two_back, "ctx")
    swap_b = swapped(jnp.where(core == 1, four_back, gated), "ctx")
    sources = [four_back, swap_b, two_back, swap_a, gated]
    lane_chunk = 128
    per_chunk = lane_chunk // group_size
    span = (lags + 1) * rows
    kernel = functools.partial(conv_kernel, lags=lags, rows=rows, group_size=group_size)
    block = pl.BlockSpec((rows, lane_chunk), lambda j, c: (0, j))
    return pl.pallas_call(
        kernel,
        grid_spec=pltpu.PrefetchScalarGridSpec(
            num_scalar_prefetch=1,
            grid=(channels // lane_chunk,),
            in_specs=[block] * (lags + 1)
            + [
                pl.BlockSpec((per_chunk, (lags + 2) * rows), lambda j, c: (j, 0)),
                pl.BlockSpec((rows, span), lambda j, c: (0, 0)),
                block,
            ],
            out_specs=block,
            scratch_shapes=[
                pltpu.VMEM((lags + 1, rows, rows * per_chunk), jnp.bfloat16),
                pltpu.VMEM((rows * per_chunk, lane_chunk), jnp.bfloat16),
            ],
        ),
        out_shape=jax.ShapeDtypeStruct((rows, channels), jnp.bfloat16),
    )(jnp.reshape(core, (1,)).astype(jnp.int32), *sources, padded, mask, queries)


def solution(mesh):
    return jax.shard_map(
        shards,
        mesh=mesh,
        in_specs=(
            P(("dp", "ctx"), None),
            P(("dp", "ctx"), None),
            P(("dp", "ctx"), None),
            P("ctx", None),
            P(("dp", "ctx")),
        ),
        out_specs=P(("dp", "ctx"), None),
        check_vma=False,
    )
```

```python
import functools

import jax
import jax.numpy as jnp
from jax import lax
from jax.experimental import pallas as pl
from jax.experimental.pallas import tpu as pltpu
from jax.sharding import PartitionSpec as P


def shifted(value, axis, steps):
    count = lax.axis_size(axis)
    first, last = (max(0, -steps), min(count, count - steps))
    return lax.ppermute(value, axis, [(source, source + steps) for source in range(first, last)])


def swapped(value, axis):
    count = lax.axis_size(axis)
    return lax.ppermute(value, axis, [(source, source ^ 1) for source in range(count)])


def conv_kernel(core_ref, *refs, lags, rows, group_size):
    g_refs = list(refs[:lags + 1])
    p_ref, m_ref, q_ref, o_ref, lhs_ref, rhs_ref = refs[lags + 1:]
    lane_chunk = rhs_ref.shape[1]
    per_chunk = lane_chunk // group_size
    row = lax.broadcasted_iota(jnp.int32, (rows, rows), 0)
    upper = lax.broadcasted_iota(jnp.int32, (rows, rows), 1) >= row
    owner = lax.broadcasted_iota(jnp.int32, (rows, lane_chunk), 1) // group_size
    even = core_ref[0] == 0
    for u in range(q_ref.shape[1] // lane_chunk):
        lanes = slice(lane_chunk * u, lane_chunk * (u + 1))
        for k in range(per_chunk):
            tap_row = p_ref[u * per_chunk + k : u * per_chunk + k + 1, :]
            rolled = [
                pltpu.roll(
                    jnp.broadcast_to(tap_row[:, rows * m : rows * (m + 1)], (rows, rows)),
                    0,
                    1,
                    stride=1,
                    stride_axis=0,
                )
                for m in range(lags + 2)
            ]
            for n in range(lags + 1):
                tile = jnp.where(upper, rolled[n + 1], rolled[n]) * m_ref[:, rows * n : rows * (n + 1)]
                lhs_ref[n, :, rows * k : rows * (k + 1)] = tile.astype(jnp.bfloat16)
        blocks = [g[:, lanes] for g in g_refs]
        near, far = blocks[lags - 1], blocks[lags - 3]
        blocks[lags - 1] = jnp.where(even, near, far)
        blocks[lags - 3] = jnp.where(even, far, near)
        acc = jnp.zeros((rows, lane_chunk), jnp.float32)
        for n in range(lags + 1):
            source = blocks[n]
            for k in range(per_chunk):
                rhs_ref[rows * k : rows * (k + 1), :] = jnp.where(owner == k, source, jnp.zeros_like(source))
            term = jnp.dot(lhs_ref[n], rhs_ref[...], preferred_element_type=jnp.float32)
            if n < lags:
                term = term.astype(jnp.bfloat16).astype(jnp.float32)
            acc = acc + term
        o_ref[:, lanes] = (q_ref[:, lanes].astype(jnp.float32) * acc).astype(o_ref.dtype)


def shards(queries, keys, values, taps, segment_ids):
    rows = queries.shape[0]
    channels = queries.shape[1]
    filters = taps.shape[1]
    group_size = channels // filters
    ctx_count = lax.axis_size("ctx")
    own_index = lax.axis_index("ctx")
    core = own_index % 2
    tap_rows = taps.shape[0]
    filt_len = tap_rows * ctx_count
    lags = filt_len // rows
    seg_row = jnp.zeros((1, filters), jnp.bfloat16).at[0, :rows].set(segment_ids.astype(jnp.bfloat16))
    packed = jnp.concatenate([taps, seg_row], axis=0)
    packed = lax.all_gather(packed, "ctx", axis=0, tiled=False)
    packed, keys, values = lax.optimization_barrier((packed, keys, values))
    all_taps = packed[:, :tap_rows].reshape(filt_len, filters).astype(jnp.float32)
    all_segs = packed[:, tap_rows, :rows].astype(jnp.int32)
    gated = (keys.astype(jnp.float32) * values.astype(jnp.float32)).astype(jnp.bfloat16)
    padded = jnp.concatenate(
        [
            jnp.zeros((filters, rows + 1), jnp.float32),
            all_taps.T[:, ::-1],
            jnp.zeros((filters, rows - 1), jnp.float32),
        ],
        axis=1,
    )
    seg_sources = [
        lax.dynamic_index_in_dim(all_segs, jnp.maximum(own_index - lag, 0), 0, keepdims=False)
        for lag in range(lags, -1, -1)
    ]
    mask = (segment_ids[:, None] == jnp.concatenate(seg_sources)[None, :]).astype(jnp.float32)
    two_back = shifted(gated, "ctx", 2)
    four_back = shifted(gated, "ctx", 4)
    swap_a = swapped(two_back, "ctx")
    swap_b = swapped(jnp.where(core == 1, four_back, gated), "ctx")
    sources = [four_back, swap_b, two_back, swap_a, gated]
    lane_chunk = 128
    per_chunk = lane_chunk // group_size
    step_lanes = lane_chunk * 4 if channels % (lane_chunk * 4) == 0 else lane_chunk
    span = (lags + 1) * rows
    kernel = functools.partial(conv_kernel, lags=lags, rows=rows, group_size=group_size)
    block = pl.BlockSpec((rows, step_lanes), lambda j, c: (0, j))
    return pl.pallas_call(
        kernel,
        grid_spec=pltpu.PrefetchScalarGridSpec(
            num_scalar_prefetch=1,
            grid=(channels // step_lanes,),
            in_specs=[block] * (lags + 1)
            + [
                pl.BlockSpec((step_lanes // group_size, (lags + 2) * rows), lambda j, c: (j, 0)),
                pl.BlockSpec((rows, span), lambda j, c: (0, 0)),
                block,
            ],
            out_specs=block,
            scratch_shapes=[
                pltpu.VMEM((lags + 1, rows, rows * per_chunk), jnp.bfloat16),
                pltpu.VMEM((rows * per_chunk, lane_chunk), jnp.bfloat16),
            ],
        ),
        out_shape=jax.ShapeDtypeStruct((rows, channels), jnp.bfloat16),
    )(jnp.reshape(core, (1,)).astype(jnp.int32), *sources, padded, mask, queries)


def solution(mesh):
    return jax.shard_map(
        shards,
        mesh=mesh,
        in_specs=(
            P(("dp", "ctx"), None),
            P(("dp", "ctx"), None),
            P(("dp", "ctx"), None),
            P("ctx", None),
            P(("dp", "ctx")),
        ),
        out_specs=P(("dp", "ctx"), None),
        check_vma=False,
    )
```

```python
import functools

import jax
import jax.numpy as jnp
from jax import lax
from jax.experimental import pallas as pl
from jax.experimental.pallas import tpu as pltpu
from jax.sharding import PartitionSpec as P


def shifted(value, axis, steps):
    count = lax.axis_size(axis)
    first, last = (max(0, -steps), min(count, count - steps))
    return lax.ppermute(value, axis, [(source, source + steps) for source in range(first, last)])


def swapped(value, axis):
    count = lax.axis_size(axis)
    return lax.ppermute(value, axis, [(source, source ^ 1) for source in range(count)])


def two_back_relayed(value, axis, own_index):
    count = lax.axis_size(axis)
    half = value.shape[0] // 2
    relay = [s for s in range(count) if s % 4 >= 2 and s + 2 < count]
    direct = [(s, s + 2) for s in range(count - 2) if s not in relay]
    plain = lax.ppermute(value, axis, direct)
    top = lax.ppermute(value[:half], axis, [(s, s + 4) for s in relay])
    top = lax.ppermute(top, axis, [(s + 4, s + 2) for s in relay])
    bottom = lax.ppermute(value[half:], axis, [(s, s - 2) for s in relay])
    bottom = lax.ppermute(bottom, axis, [(s - 2, s + 2) for s in relay])
    relayed = jnp.isin(own_index, jnp.array([s + 2 for s in relay] or [-1], jnp.int32))
    return jnp.where(relayed, jnp.concatenate([top, bottom], axis=0), plain)


def conv_kernel(core_ref, *refs, lags, rows, group_size):
    g_refs = list(refs[:lags + 1])
    p_ref, m_ref, q_ref, o_ref, lhs_ref, rhs_ref = refs[lags + 1:]
    lane_chunk = rhs_ref.shape[1]
    per_chunk = lane_chunk // group_size
    row = lax.broadcasted_iota(jnp.int32, (rows, rows), 0)
    upper = lax.broadcasted_iota(jnp.int32, (rows, rows), 1) >= row
    owner = lax.broadcasted_iota(jnp.int32, (rows, lane_chunk), 1) // group_size
    even = core_ref[0] == 0
    for u in range(q_ref.shape[1] // lane_chunk):
        lanes = slice(lane_chunk * u, lane_chunk * (u + 1))
        for k in range(per_chunk):
            tap_row = p_ref[u * per_chunk + k : u * per_chunk + k + 1, :]
            rolled = [
                pltpu.roll(
                    jnp.broadcast_to(tap_row[:, rows * m : rows * (m + 1)], (rows, rows)),
                    0,
                    1,
                    stride=1,
                    stride_axis=0,
                )
                for m in range(lags + 2)
            ]
            for n in range(lags + 1):
                tile = jnp.where(upper, rolled[n + 1], rolled[n]) * m_ref[:, rows * n : rows * (n + 1)]
                lhs_ref[n, :, rows * k : rows * (k + 1)] = tile.astype(jnp.bfloat16)
        blocks = [g[:, lanes] for g in g_refs]
        near, far = blocks[lags - 1], blocks[lags - 3]
        blocks[lags - 1] = jnp.where(even, near, far)
        blocks[lags - 3] = jnp.where(even, far, near)
        acc = jnp.zeros((rows, lane_chunk), jnp.float32)
        for n in range(lags + 1):
            source = blocks[n]
            for k in range(per_chunk):
                rhs_ref[rows * k : rows * (k + 1), :] = jnp.where(owner == k, source, jnp.zeros_like(source))
            term = jnp.dot(lhs_ref[n], rhs_ref[...], preferred_element_type=jnp.float32)
            if n < lags:
                term = term.astype(jnp.bfloat16).astype(jnp.float32)
            acc = acc + term
        o_ref[:, lanes] = (q_ref[:, lanes].astype(jnp.float32) * acc).astype(o_ref.dtype)


def shards(queries, keys, values, taps, segment_ids):
    rows = queries.shape[0]
    channels = queries.shape[1]
    filters = taps.shape[1]
    group_size = channels // filters
    ctx_count = lax.axis_size("ctx")
    own_index = lax.axis_index("ctx")
    core = own_index % 2
    tap_rows = taps.shape[0]
    filt_len = tap_rows * ctx_count
    lags = filt_len // rows
    seg_row = jnp.zeros((1, filters), jnp.bfloat16).at[0, :rows].set(segment_ids.astype(jnp.bfloat16))
    packed = jnp.concatenate([taps, seg_row], axis=0)
    packed = lax.all_gather(packed, "ctx", axis=0, tiled=False)
    packed, keys, values = lax.optimization_barrier((packed, keys, values))
    all_taps = packed[:, :tap_rows].reshape(filt_len, filters).astype(jnp.float32)
    all_segs = packed[:, tap_rows, :rows].astype(jnp.int32)
    gated = (keys.astype(jnp.float32) * values.astype(jnp.float32)).astype(jnp.bfloat16)
    padded = jnp.concatenate(
        [
            jnp.zeros((filters, rows + 1), jnp.float32),
            all_taps.T[:, ::-1],
            jnp.zeros((filters, rows - 1), jnp.float32),
        ],
        axis=1,
    )
    seg_sources = [
        lax.dynamic_index_in_dim(all_segs, jnp.maximum(own_index - lag, 0), 0, keepdims=False)
        for lag in range(lags, -1, -1)
    ]
    mask = (segment_ids[:, None] == jnp.concatenate(seg_sources)[None, :]).astype(jnp.float32)
    two_back = two_back_relayed(gated, "ctx", own_index)
    four_back = shifted(gated, "ctx", 4)
    swap_a = swapped(two_back, "ctx")
    swap_b = swapped(jnp.where(core == 1, four_back, gated), "ctx")
    sources = [four_back, swap_b, two_back, swap_a, gated]
    lane_chunk = 128
    per_chunk = lane_chunk // group_size
    step_lanes = lane_chunk * 4 if channels % (lane_chunk * 4) == 0 else lane_chunk
    span = (lags + 1) * rows
    kernel = functools.partial(conv_kernel, lags=lags, rows=rows, group_size=group_size)
    block = pl.BlockSpec((rows, step_lanes), lambda j, c: (0, j))
    return pl.pallas_call(
        kernel,
        grid_spec=pltpu.PrefetchScalarGridSpec(
            num_scalar_prefetch=1,
            grid=(channels // step_lanes,),
            in_specs=[block] * (lags + 1)
            + [
                pl.BlockSpec((step_lanes // group_size, (lags + 2) * rows), lambda j, c: (j, 0)),
                pl.BlockSpec((rows, span), lambda j, c: (0, 0)),
                block,
            ],
            out_specs=block,
            scratch_shapes=[
                pltpu.VMEM((lags + 1, rows, rows * per_chunk), jnp.bfloat16),
                pltpu.VMEM((rows * per_chunk, lane_chunk), jnp.bfloat16),
            ],
        ),
        out_shape=jax.ShapeDtypeStruct((rows, channels), jnp.bfloat16),
    )(jnp.reshape(core, (1,)).astype(jnp.int32), *sources, padded, mask, queries)


def solution(mesh):
    return jax.shard_map(
        shards,
        mesh=mesh,
        in_specs=(
            P(("dp", "ctx"), None),
            P(("dp", "ctx"), None),
            P(("dp", "ctx"), None),
            P("ctx", None),
            P(("dp", "ctx")),
        ),
        out_specs=P(("dp", "ctx"), None),
        check_vma=False,
    )
```

```python
import functools

import jax
import jax.numpy as jnp
from jax import lax
from jax.experimental import pallas as pl
from jax.experimental.pallas import tpu as pltpu
from jax.sharding import PartitionSpec as P


def shifted(value, axis, steps):
    count = lax.axis_size(axis)
    first, last = (max(0, -steps), min(count, count - steps))
    return lax.ppermute(value, axis, [(source, source + steps) for source in range(first, last)])


def swapped(value, axis):
    count = lax.axis_size(axis)
    return lax.ppermute(value, axis, [(source, source ^ 1) for source in range(count)])


def conv_kernel(*refs, count, rows, group_size, rounded, first, final):
    g_refs = refs[:count]
    w_refs = refs[count : 2 * count]
    rest = list(refs[2 * count :])
    m_ref = rest.pop(0)
    acc_ref = None if first else rest.pop(0)
    q_ref = rest.pop(0) if final else None
    o_ref, lhs_ref, rhs_ref = rest
    lane_chunk = rhs_ref.shape[1]
    per_chunk = lane_chunk // group_size
    row = lax.broadcasted_iota(jnp.int32, (rows, rows), 0)
    upper = lax.broadcasted_iota(jnp.int32, (rows, rows), 1) >= row
    owner = lax.broadcasted_iota(jnp.int32, (rows, lane_chunk), 1) // group_size
    for u in range(o_ref.shape[1] // lane_chunk):
        lanes = slice(lane_chunk * u, lane_chunk * (u + 1))
        for n in range(count):
            for k in range(per_chunk):
                window = w_refs[n][u * per_chunk + k : u * per_chunk + k + 1, :]
                lo, hi = [
                    pltpu.roll(
                        jnp.broadcast_to(window[:, rows * m : rows * (m + 1)], (rows, rows)),
                        0,
                        1,
                        stride=1,
                        stride_axis=0,
                    )
                    for m in range(2)
                ]
                tile = jnp.where(upper, hi, lo) * m_ref[:, rows * n : rows * (n + 1)]
                lhs_ref[n, :, rows * k : rows * (k + 1)] = tile.astype(jnp.bfloat16)
        acc = jnp.zeros((rows, lane_chunk), jnp.float32) if first else acc_ref[:, lanes]
        for n in range(count):
            source = g_refs[n][:, lanes]
            for k in range(per_chunk):
                rhs_ref[rows * k : rows * (k + 1), :] = jnp.where(owner == k, source, jnp.zeros_like(source))
            term = jnp.dot(lhs_ref[n], rhs_ref[...], preferred_element_type=jnp.float32)
            if rounded[n]:
                term = term.astype(jnp.bfloat16).astype(jnp.float32)
            acc = acc + term
        if final:
            o_ref[:, lanes] = (q_ref[:, lanes].astype(jnp.float32) * acc).astype(o_ref.dtype)
        else:
            o_ref[:, lanes] = acc


def conv_terms(sources, windows, mask, rounded, acc, queries, group_size):
    rows, channels = sources[0].shape
    count = len(sources)
    first = acc is None
    final = queries is not None
    lane_chunk = 128
    step_lanes = lane_chunk * 4 if channels % (lane_chunk * 4) == 0 else lane_chunk
    block = pl.BlockSpec((rows, step_lanes), lambda j: (0, j))
    window_spec = pl.BlockSpec((step_lanes // group_size, 2 * rows), lambda j: (j, 0))
    in_specs = [block] * count + [window_spec] * count + [pl.BlockSpec((rows, count * rows), lambda j: (0, 0))]
    operands = list(sources) + list(windows) + [mask]
    if not first:
        in_specs.append(block)
        operands.append(acc)
    if final:
        in_specs.append(block)
        operands.append(queries)
    kernel = functools.partial(
        conv_kernel, count=count, rows=rows, group_size=group_size, rounded=tuple(rounded), first=first, final=final
    )
    return pl.pallas_call(
        kernel,
        grid=(channels // step_lanes,),
        in_specs=in_specs,
        out_specs=block,
        scratch_shapes=[
            pltpu.VMEM((count, rows, rows * (lane_chunk // group_size)), jnp.bfloat16),
            pltpu.VMEM((rows * (lane_chunk // group_size), lane_chunk), jnp.bfloat16),
        ],
        out_shape=jax.ShapeDtypeStruct((rows, channels), jnp.bfloat16 if final else jnp.float32),
    )(*operands)


def shards(queries, keys, values, taps, segment_ids):
    rows = queries.shape[0]
    channels = queries.shape[1]
    filters = taps.shape[1]
    group_size = channels // filters
    ctx_count = lax.axis_size("ctx")
    own_index = lax.axis_index("ctx")
    core = own_index % 2
    tap_rows = taps.shape[0]
    filt_len = tap_rows * ctx_count
    lags = filt_len // rows
    seg_row = jnp.zeros((1, filters), jnp.bfloat16).at[0, :rows].set(segment_ids.astype(jnp.bfloat16))
    packed = jnp.concatenate([taps, seg_row], axis=0)
    packed = lax.all_gather(packed, "ctx", axis=0, tiled=False)
    packed, keys, values = lax.optimization_barrier((packed, keys, values))
    all_taps = packed[:, :tap_rows].reshape(filt_len, filters).astype(jnp.float32)
    all_segs = packed[:, tap_rows, :rows].astype(jnp.int32)
    gated = (keys.astype(jnp.float32) * values.astype(jnp.float32)).astype(jnp.bfloat16)
    padded = jnp.concatenate(
        [
            jnp.zeros((filters, rows + 1), jnp.float32),
            all_taps.T[:, ::-1],
            jnp.zeros((filters, rows - 1), jnp.float32),
        ],
        axis=1,
    )

    def window(lag):
        return lax.dynamic_slice_in_dim(padded, (lags - lag) * rows, 2 * rows, 1)

    def mask_for(lags_here):
        segs = [
            lax.dynamic_index_in_dim(all_segs, jnp.maximum(own_index - lag, 0), 0, keepdims=False)
            for lag in lags_here
        ]
        return (segment_ids[:, None] == jnp.concatenate(segs)[None, :]).astype(jnp.float32)

    two_back = shifted(gated, "ctx", 2)
    four_back = shifted(gated, "ctx", 4)
    swap_a = swapped(two_back, "ctx")
    swap_b = swapped(jnp.where(core == 1, four_back, gated), "ctx")
    lag_a = 1 + 2 * core
    lag_b = 3 - 2 * core
    first_lags = [jnp.int32(0), jnp.int32(2), lag_a]
    acc = conv_terms(
        [gated, two_back, swap_a], [window(lag) for lag in first_lags], mask_for(first_lags),
        [False, True, True], None, None, group_size,
    )
    last_lags = [jnp.int32(4), lag_b]
    return conv_terms(
        [four_back, swap_b], [window(lag) for lag in last_lags], mask_for(last_lags),
        [True, True], acc, queries, group_size,
    )


def solution(mesh):
    return jax.shard_map(
        shards,
        mesh=mesh,
        in_specs=(
            P(("dp", "ctx"), None),
            P(("dp", "ctx"), None),
            P(("dp", "ctx"), None),
            P("ctx", None),
            P(("dp", "ctx")),
        ),
        out_specs=P(("dp", "ctx"), None),
        check_vma=False,
    )
```

```python
import functools

import jax
import jax.numpy as jnp
from jax import lax
from jax.experimental import pallas as pl
from jax.experimental.pallas import tpu as pltpu
from jax.sharding import PartitionSpec as P


def shifted(value, axis, steps):
    count = lax.axis_size(axis)
    first, last = (max(0, -steps), min(count, count - steps))
    return lax.ppermute(value, axis, [(source, source + steps) for source in range(first, last)])


def swapped(value, axis):
    count = lax.axis_size(axis)
    return lax.ppermute(value, axis, [(source, source ^ 1) for source in range(count)])


def conv_kernel(core_ref, *refs, lags, rows, group_size):
    g_refs = list(refs[:lags + 1])
    p_ref, m_ref, q_ref, o_ref, lhs_ref, rhs_ref = refs[lags + 1:]
    lane_chunk = rhs_ref.shape[1]
    per_chunk = lane_chunk // group_size
    row = lax.broadcasted_iota(jnp.int32, (rows, rows), 0)
    upper = lax.broadcasted_iota(jnp.int32, (rows, rows), 1) >= row
    owner = lax.broadcasted_iota(jnp.int32, (rows, lane_chunk), 1) // group_size
    even = core_ref[0] == 0
    for u in range(q_ref.shape[1] // lane_chunk):
        lanes = slice(lane_chunk * u, lane_chunk * (u + 1))
        for k in range(per_chunk):
            tap_row = p_ref[u * per_chunk + k : u * per_chunk + k + 1, :]
            rolled = [
                pltpu.roll(
                    jnp.broadcast_to(tap_row[:, rows * m : rows * (m + 1)], (rows, rows)),
                    0,
                    1,
                    stride=1,
                    stride_axis=0,
                )
                for m in range(lags + 2)
            ]
            for n in range(lags + 1):
                tile = jnp.where(upper, rolled[n + 1], rolled[n]) * m_ref[:, rows * n : rows * (n + 1)]
                lhs_ref[n, :, rows * k : rows * (k + 1)] = tile.astype(jnp.bfloat16)
        blocks = [g[:, lanes] for g in g_refs]
        near, far = blocks[lags - 1], blocks[lags - 3]
        blocks[lags - 1] = jnp.where(even, near, far)
        blocks[lags - 3] = jnp.where(even, far, near)
        acc = jnp.zeros((rows, lane_chunk), jnp.float32)
        for n in range(lags + 1):
            source = blocks[n]
            for k in range(per_chunk):
                rhs_ref[rows * k : rows * (k + 1), :] = jnp.where(owner == k, source, jnp.zeros_like(source))
            term = jnp.dot(lhs_ref[n], rhs_ref[...], preferred_element_type=jnp.float32)
            if n < lags:
                term = term.astype(jnp.bfloat16).astype(jnp.float32)
            acc = acc + term
        o_ref[:, lanes] = (q_ref[:, lanes].astype(jnp.float32) * acc).astype(o_ref.dtype)


def shards(queries, keys, values, taps, segment_ids):
    rows = queries.shape[0]
    channels = queries.shape[1]
    filters = taps.shape[1]
    group_size = channels // filters
    ctx_count = lax.axis_size("ctx")
    own_index = lax.axis_index("ctx")
    core = own_index % 2
    tap_rows = taps.shape[0]
    filt_len = tap_rows * ctx_count
    lags = filt_len // rows
    seg_row = jnp.zeros((1, filters), jnp.bfloat16).at[0, :rows].set(segment_ids.astype(jnp.bfloat16))
    packed = jnp.concatenate([taps, seg_row], axis=0)
    gated = (keys.astype(jnp.float32) * values.astype(jnp.float32)).astype(jnp.bfloat16)
    packed, gated = lax.optimization_barrier((packed, gated))
    two_back = shifted(gated, "ctx", 2)
    four_back = shifted(gated, "ctx", 4)
    packed = lax.all_gather(packed, "ctx", axis=0, tiled=False)
    all_taps = packed[:, :tap_rows].reshape(filt_len, filters).astype(jnp.float32)
    all_segs = packed[:, tap_rows, :rows].astype(jnp.int32)
    padded = jnp.concatenate(
        [
            jnp.zeros((filters, rows + 1), jnp.float32),
            all_taps.T[:, ::-1],
            jnp.zeros((filters, rows - 1), jnp.float32),
        ],
        axis=1,
    )
    seg_sources = [
        lax.dynamic_index_in_dim(all_segs, jnp.maximum(own_index - lag, 0), 0, keepdims=False)
        for lag in range(lags, -1, -1)
    ]
    mask = (segment_ids[:, None] == jnp.concatenate(seg_sources)[None, :]).astype(jnp.float32)
    swap_a = swapped(two_back, "ctx")
    swap_b = swapped(jnp.where(core == 1, four_back, gated), "ctx")
    sources = [four_back, swap_b, two_back, swap_a, gated]
    lane_chunk = 128
    per_chunk = lane_chunk // group_size
    step_lanes = lane_chunk * 4 if channels % (lane_chunk * 4) == 0 else lane_chunk
    span = (lags + 1) * rows
    kernel = functools.partial(conv_kernel, lags=lags, rows=rows, group_size=group_size)
    block = pl.BlockSpec((rows, step_lanes), lambda j, c: (0, j))
    return pl.pallas_call(
        kernel,
        grid_spec=pltpu.PrefetchScalarGridSpec(
            num_scalar_prefetch=1,
            grid=(channels // step_lanes,),
            in_specs=[block] * (lags + 1)
            + [
                pl.BlockSpec((step_lanes // group_size, (lags + 2) * rows), lambda j, c: (j, 0)),
                pl.BlockSpec((rows, span), lambda j, c: (0, 0)),
                block,
            ],
            out_specs=block,
            scratch_shapes=[
                pltpu.VMEM((lags + 1, rows, rows * per_chunk), jnp.bfloat16),
                pltpu.VMEM((rows * per_chunk, lane_chunk), jnp.bfloat16),
            ],
        ),
        out_shape=jax.ShapeDtypeStruct((rows, channels), jnp.bfloat16),
    )(jnp.reshape(core, (1,)).astype(jnp.int32), *sources, padded, mask, queries)


def solution(mesh):
    return jax.shard_map(
        shards,
        mesh=mesh,
        in_specs=(
            P(("dp", "ctx"), None),
            P(("dp", "ctx"), None),
            P(("dp", "ctx"), None),
            P("ctx", None),
            P(("dp", "ctx")),
        ),
        out_specs=P(("dp", "ctx"), None),
        check_vma=False,
    )
```

```python
import functools

import jax
import jax.numpy as jnp
from jax import lax
from jax.experimental import pallas as pl
from jax.experimental.pallas import tpu as pltpu
from jax.sharding import PartitionSpec as P


def shifted(value, axis, steps):
    count = lax.axis_size(axis)
    first, last = (max(0, -steps), min(count, count - steps))
    return lax.ppermute(value, axis, [(source, source + steps) for source in range(first, last)])


def swapped(value, axis):
    count = lax.axis_size(axis)
    return lax.ppermute(value, axis, [(source, source ^ 1) for source in range(count)])


def weight_kernel(p_ref, m_ref, w_ref, *, lags, rows):
    row = lax.broadcasted_iota(jnp.int32, (rows, rows), 0)
    upper = lax.broadcasted_iota(jnp.int32, (rows, rows), 1) >= row
    for k in range(p_ref.shape[0]):
        tap_row = p_ref[k : k + 1, :]
        rolled = [
            pltpu.roll(
                jnp.broadcast_to(tap_row[:, rows * m : rows * (m + 1)], (rows, rows)),
                0,
                1,
                stride=1,
                stride_axis=0,
            )
            for m in range(lags + 2)
        ]
        for n in range(lags + 1):
            tile = jnp.where(upper, rolled[n + 1], rolled[n]) * m_ref[:, rows * n : rows * (n + 1)]
            w_ref[n, :, rows * k : rows * (k + 1)] = tile.astype(jnp.bfloat16)


def conv_kernel(core_ref, *refs, lags, rows, group_size):
    g_refs = list(refs[:lags + 1])
    w_ref, q_ref, o_ref, rhs_ref = refs[lags + 1:]
    lane_chunk = rhs_ref.shape[1]
    per_chunk = lane_chunk // group_size
    owner = lax.broadcasted_iota(jnp.int32, (rows, lane_chunk), 1) // group_size
    even = core_ref[0] == 0
    for u in range(q_ref.shape[1] // lane_chunk):
        lanes = slice(lane_chunk * u, lane_chunk * (u + 1))
        blocks = [g[:, lanes] for g in g_refs]
        near, far = blocks[lags - 1], blocks[lags - 3]
        blocks[lags - 1] = jnp.where(even, near, far)
        blocks[lags - 3] = jnp.where(even, far, near)
        acc = jnp.zeros((rows, lane_chunk), jnp.float32)
        for n in range(lags + 1):
            source = blocks[n]
            for k in range(per_chunk):
                rhs_ref[rows * k : rows * (k + 1), :] = jnp.where(owner == k, source, jnp.zeros_like(source))
            weights = w_ref[n, :, rows * per_chunk * u : rows * per_chunk * (u + 1)]
            term = jnp.dot(weights, rhs_ref[...], preferred_element_type=jnp.float32)
            if n < lags:
                term = term.astype(jnp.bfloat16).astype(jnp.float32)
            acc = acc + term
        o_ref[:, lanes] = (q_ref[:, lanes].astype(jnp.float32) * acc).astype(o_ref.dtype)


def shards(queries, keys, values, taps, segment_ids):
    rows = queries.shape[0]
    channels = queries.shape[1]
    filters = taps.shape[1]
    group_size = channels // filters
    ctx_count = lax.axis_size("ctx")
    own_index = lax.axis_index("ctx")
    core = own_index % 2
    tap_rows = taps.shape[0]
    filt_len = tap_rows * ctx_count
    lags = filt_len // rows
    seg_row = jnp.zeros((1, filters), jnp.bfloat16).at[0, :rows].set(segment_ids.astype(jnp.bfloat16))
    packed = jnp.concatenate([taps, seg_row], axis=0)
    packed = lax.all_gather(packed, "ctx", axis=0, tiled=False)
    packed, keys, values = lax.optimization_barrier((packed, keys, values))
    all_taps = packed[:, :tap_rows].reshape(filt_len, filters).astype(jnp.float32)
    all_segs = packed[:, tap_rows, :rows].astype(jnp.int32)
    gated = (keys.astype(jnp.float32) * values.astype(jnp.float32)).astype(jnp.bfloat16)
    padded = jnp.concatenate(
        [
            jnp.zeros((filters, rows + 1), jnp.float32),
            all_taps.T[:, ::-1],
            jnp.zeros((filters, rows - 1), jnp.float32),
        ],
        axis=1,
    )
    seg_sources = [
        lax.dynamic_index_in_dim(all_segs, jnp.maximum(own_index - lag, 0), 0, keepdims=False)
        for lag in range(lags, -1, -1)
    ]
    mask = (segment_ids[:, None] == jnp.concatenate(seg_sources)[None, :]).astype(jnp.float32)
    two_back = shifted(gated, "ctx", 2)
    four_back = shifted(gated, "ctx", 4)
    lane_chunk = 128
    step_lanes = lane_chunk * 4 if channels % (lane_chunk * 4) == 0 else lane_chunk
    span = (lags + 1) * rows
    step_filters = step_lanes // group_size
    weights = pl.pallas_call(
        functools.partial(weight_kernel, lags=lags, rows=rows),
        grid=(channels // step_lanes,),
        in_specs=[
            pl.BlockSpec((step_filters, (lags + 2) * rows), lambda j: (j, 0)),
            pl.BlockSpec((rows, span), lambda j: (0, 0)),
        ],
        out_specs=pl.BlockSpec((lags + 1, rows, step_filters * rows), lambda j: (0, 0, j)),
        out_shape=jax.ShapeDtypeStruct((lags + 1, rows, filters * rows), jnp.bfloat16),
        cost_estimate=pl.CostEstimate(
            flops=8 * (lags + 1) * rows * rows * filters,
            transcendentals=0,
            bytes_accessed=2 * (lags + 1) * rows * rows * filters,
        ),
    )(padded, mask)
    weights, two_back, four_back = lax.optimization_barrier((weights, two_back, four_back))
    swap_a = swapped(two_back, "ctx")
    swap_b = swapped(jnp.where(core == 1, four_back, gated), "ctx")
    sources = [four_back, swap_b, two_back, swap_a, gated]
    kernel = functools.partial(conv_kernel, lags=lags, rows=rows, group_size=group_size)
    block = pl.BlockSpec((rows, step_lanes), lambda j, c: (0, j))
    return pl.pallas_call(
        kernel,
        grid_spec=pltpu.PrefetchScalarGridSpec(
            num_scalar_prefetch=1,
            grid=(channels // step_lanes,),
            in_specs=[block] * (lags + 1)
            + [
                pl.BlockSpec((lags + 1, rows, step_filters * rows), lambda j, c: (0, 0, j)),
                block,
            ],
            out_specs=block,
            scratch_shapes=[pltpu.VMEM((rows * (lane_chunk // group_size), lane_chunk), jnp.bfloat16)],
        ),
        out_shape=jax.ShapeDtypeStruct((rows, channels), jnp.bfloat16),
    )(jnp.reshape(core, (1,)).astype(jnp.int32), *sources, weights, queries)


def solution(mesh):
    return jax.shard_map(
        shards,
        mesh=mesh,
        in_specs=(
            P(("dp", "ctx"), None),
            P(("dp", "ctx"), None),
            P(("dp", "ctx"), None),
            P("ctx", None),
            P(("dp", "ctx")),
        ),
        out_specs=P(("dp", "ctx"), None),
        check_vma=False,
    )
```

```python
import functools

import jax
import jax.numpy as jnp
from jax import lax
from jax.experimental import pallas as pl
from jax.experimental.pallas import tpu as pltpu
from jax.sharding import PartitionSpec as P


def shifted(value, axis, steps):
    count = lax.axis_size(axis)
    first, last = (max(0, -steps), min(count, count - steps))
    return lax.ppermute(value, axis, [(source, source + steps) for source in range(first, last)])


def swapped(value, axis):
    count = lax.axis_size(axis)
    return lax.ppermute(value, axis, [(source, source ^ 1) for source in range(count)])


def weight_kernel(p_ref, m_ref, g_ref, w_ref, a_ref, lhs_ref, rhs_ref, *, lags, rows, group_size):
    row = lax.broadcasted_iota(jnp.int32, (rows, rows), 0)
    upper = lax.broadcasted_iota(jnp.int32, (rows, rows), 1) >= row
    lane_chunk = rhs_ref.shape[1]
    per_chunk = lane_chunk // group_size
    owner = lax.broadcasted_iota(jnp.int32, (rows, lane_chunk), 1) // group_size
    for u in range(g_ref.shape[1] // lane_chunk):
        for j in range(per_chunk):
            k = u * per_chunk + j
            tap_row = p_ref[k : k + 1, :]
            rolled = [
                pltpu.roll(
                    jnp.broadcast_to(tap_row[:, rows * m : rows * (m + 1)], (rows, rows)),
                    0,
                    1,
                    stride=1,
                    stride_axis=0,
                )
                for m in range(lags + 2)
            ]
            for n in range(lags + 1):
                tile = jnp.where(upper, rolled[n + 1], rolled[n]) * m_ref[:, rows * n : rows * (n + 1)]
                if n < lags:
                    w_ref[n, :, rows * k : rows * (k + 1)] = tile.astype(jnp.bfloat16)
                else:
                    lhs_ref[:, rows * j : rows * (j + 1)] = tile.astype(jnp.bfloat16)
        lanes = slice(lane_chunk * u, lane_chunk * (u + 1))
        source = g_ref[:, lanes]
        for j in range(per_chunk):
            rhs_ref[rows * j : rows * (j + 1), :] = jnp.where(owner == j, source, jnp.zeros_like(source))
        a_ref[:, lanes] = jnp.dot(lhs_ref[...], rhs_ref[...], preferred_element_type=jnp.float32)


def conv_kernel(core_ref, *refs, lags, rows, group_size):
    g_refs = list(refs[:lags])
    w_ref, a_ref, q_ref, o_ref, rhs_ref = refs[lags:]
    lane_chunk = rhs_ref.shape[1]
    per_chunk = lane_chunk // group_size
    owner = lax.broadcasted_iota(jnp.int32, (rows, lane_chunk), 1) // group_size
    even = core_ref[0] == 0
    for u in range(q_ref.shape[1] // lane_chunk):
        lanes = slice(lane_chunk * u, lane_chunk * (u + 1))
        blocks = [g[:, lanes] for g in g_refs]
        near, far = blocks[lags - 1], blocks[lags - 3]
        blocks[lags - 1] = jnp.where(even, near, far)
        blocks[lags - 3] = jnp.where(even, far, near)
        acc = a_ref[:, lanes]
        for n in range(lags):
            source = blocks[n]
            for k in range(per_chunk):
                rhs_ref[rows * k : rows * (k + 1), :] = jnp.where(owner == k, source, jnp.zeros_like(source))
            weights = w_ref[n, :, rows * per_chunk * u : rows * per_chunk * (u + 1)]
            term = jnp.dot(weights, rhs_ref[...], preferred_element_type=jnp.float32)
            acc = acc + term.astype(jnp.bfloat16).astype(jnp.float32)
        o_ref[:, lanes] = (q_ref[:, lanes].astype(jnp.float32) * acc).astype(o_ref.dtype)


def shards(queries, keys, values, taps, segment_ids):
    rows = queries.shape[0]
    channels = queries.shape[1]
    filters = taps.shape[1]
    group_size = channels // filters
    ctx_count = lax.axis_size("ctx")
    own_index = lax.axis_index("ctx")
    core = own_index % 2
    tap_rows = taps.shape[0]
    filt_len = tap_rows * ctx_count
    lags = filt_len // rows
    seg_row = jnp.zeros((1, filters), jnp.bfloat16).at[0, :rows].set(segment_ids.astype(jnp.bfloat16))
    packed = jnp.concatenate([taps, seg_row], axis=0)
    packed = lax.all_gather(packed, "ctx", axis=0, tiled=False)
    packed, keys, values = lax.optimization_barrier((packed, keys, values))
    all_taps = packed[:, :tap_rows].reshape(filt_len, filters).astype(jnp.float32)
    all_segs = packed[:, tap_rows, :rows].astype(jnp.int32)
    gated = (keys.astype(jnp.float32) * values.astype(jnp.float32)).astype(jnp.bfloat16)
    padded = jnp.concatenate(
        [
            jnp.zeros((filters, rows + 1), jnp.float32),
            all_taps.T[:, ::-1],
            jnp.zeros((filters, rows - 1), jnp.float32),
        ],
        axis=1,
    )
    seg_sources = [
        lax.dynamic_index_in_dim(all_segs, jnp.maximum(own_index - lag, 0), 0, keepdims=False)
        for lag in range(lags, -1, -1)
    ]
    mask = (segment_ids[:, None] == jnp.concatenate(seg_sources)[None, :]).astype(jnp.float32)
    two_back = shifted(gated, "ctx", 2)
    four_back = shifted(gated, "ctx", 4)
    lane_chunk = 128
    step_lanes = lane_chunk * 4 if channels % (lane_chunk * 4) == 0 else lane_chunk
    span = (lags + 1) * rows
    step_filters = step_lanes // group_size
    weights, own_term = pl.pallas_call(
        functools.partial(weight_kernel, lags=lags, rows=rows, group_size=group_size),
        grid=(channels // step_lanes,),
        in_specs=[
            pl.BlockSpec((step_filters, (lags + 2) * rows), lambda j: (j, 0)),
            pl.BlockSpec((rows, span), lambda j: (0, 0)),
            pl.BlockSpec((rows, step_lanes), lambda j: (0, j)),
        ],
        out_specs=[
            pl.BlockSpec((lags, rows, step_filters * rows), lambda j: (0, 0, j)),
            pl.BlockSpec((rows, step_lanes), lambda j: (0, j)),
        ],
        out_shape=[
            jax.ShapeDtypeStruct((lags, rows, filters * rows), jnp.bfloat16),
            jax.ShapeDtypeStruct((rows, channels), jnp.float32),
        ],
        scratch_shapes=[
            pltpu.VMEM((rows, rows * (lane_chunk // group_size)), jnp.bfloat16),
            pltpu.VMEM((rows * (lane_chunk // group_size), lane_chunk), jnp.bfloat16),
        ],
    )(padded, mask, gated)
    weights, own_term, two_back, four_back = lax.optimization_barrier((weights, own_term, two_back, four_back))
    swap_a = swapped(two_back, "ctx")
    swap_b = swapped(jnp.where(core == 1, four_back, gated), "ctx")
    sources = [four_back, swap_b, two_back, swap_a]
    kernel = functools.partial(conv_kernel, lags=lags, rows=rows, group_size=group_size)
    block = pl.BlockSpec((rows, step_lanes), lambda j, c: (0, j))
    return pl.pallas_call(
        kernel,
        grid_spec=pltpu.PrefetchScalarGridSpec(
            num_scalar_prefetch=1,
            grid=(channels // step_lanes,),
            in_specs=[block] * lags
            + [
                pl.BlockSpec((lags, rows, step_filters * rows), lambda j, c: (0, 0, j)),
                block,
                block,
            ],
            out_specs=block,
            scratch_shapes=[pltpu.VMEM((rows * (lane_chunk // group_size), lane_chunk), jnp.bfloat16)],
        ),
        out_shape=jax.ShapeDtypeStruct((rows, channels), jnp.bfloat16),
    )(jnp.reshape(core, (1,)).astype(jnp.int32), *sources, weights, own_term, queries)


def solution(mesh):
    return jax.shard_map(
        shards,
        mesh=mesh,
        in_specs=(
            P(("dp", "ctx"), None),
            P(("dp", "ctx"), None),
            P(("dp", "ctx"), None),
            P("ctx", None),
            P(("dp", "ctx")),
        ),
        out_specs=P(("dp", "ctx"), None),
        check_vma=False,
    )
```

```python
import functools

import jax
import jax.numpy as jnp
from jax import lax
from jax.experimental import pallas as pl
from jax.experimental.pallas import tpu as pltpu
from jax.sharding import PartitionSpec as P


def shifted(value, axis, steps):
    count = lax.axis_size(axis)
    first, last = (max(0, -steps), min(count, count - steps))
    return lax.ppermute(value, axis, [(source, source + steps) for source in range(first, last)])


def swapped(value, axis):
    count = lax.axis_size(axis)
    return lax.ppermute(value, axis, [(source, source ^ 1) for source in range(count)])


def weight_kernel(p_ref, m_ref, g_ref, w_ref, a_ref, lhs_ref, rhs_ref, *, lags, rows, group_size):
    row = lax.broadcasted_iota(jnp.int32, (rows, rows), 0)
    upper = lax.broadcasted_iota(jnp.int32, (rows, rows), 1) >= row
    lane_chunk = rhs_ref.shape[1]
    per_chunk = lane_chunk // group_size
    owner = lax.broadcasted_iota(jnp.int32, (rows, lane_chunk), 1) // group_size
    for u in range(g_ref.shape[1] // lane_chunk):
        for j in range(per_chunk):
            k = u * per_chunk + j
            tap_row = p_ref[k : k + 1, :]
            rolled = [
                pltpu.roll(
                    jnp.broadcast_to(tap_row[:, rows * m : rows * (m + 1)], (rows, rows)),
                    0,
                    1,
                    stride=1,
                    stride_axis=0,
                )
                for m in range(lags + 2)
            ]
            for n in range(lags + 1):
                tile = jnp.where(upper, rolled[n + 1], rolled[n]) * m_ref[:, rows * n : rows * (n + 1)]
                if n < lags:
                    w_ref[n, :, rows * k : rows * (k + 1)] = tile.astype(jnp.bfloat16)
                else:
                    lhs_ref[:, rows * j : rows * (j + 1)] = tile.astype(jnp.bfloat16)
        lanes = slice(lane_chunk * u, lane_chunk * (u + 1))
        source = g_ref[:, lanes]
        for j in range(per_chunk):
            rhs_ref[rows * j : rows * (j + 1), :] = jnp.where(owner == j, source, jnp.zeros_like(source))
        a_ref[:, lanes] = jnp.dot(lhs_ref[...], rhs_ref[...], preferred_element_type=jnp.float32)


def conv_kernel(core_ref, *refs, lags, rows, group_size):
    g_refs = list(refs[:lags])
    own_ref, w_ref, a_ref, q_ref, o_ref, rhs_ref = refs[lags:]
    lane_chunk = rhs_ref.shape[1]
    per_chunk = lane_chunk // group_size
    owner = lax.broadcasted_iota(jnp.int32, (rows, lane_chunk), 1) // group_size
    even = core_ref[0] == 0
    for u in range(q_ref.shape[1] // lane_chunk):
        lanes = slice(lane_chunk * u, lane_chunk * (u + 1))
        blocks = [g[:, lanes] for g in g_refs]
        blocks[lags - 3] = jnp.where(even, blocks[lags - 3], own_ref[:, lanes])
        near, far = blocks[lags - 1], blocks[lags - 3]
        blocks[lags - 1] = jnp.where(even, near, far)
        blocks[lags - 3] = jnp.where(even, far, near)
        acc = a_ref[:, lanes]
        for n in range(lags):
            source = blocks[n]
            for k in range(per_chunk):
                rhs_ref[rows * k : rows * (k + 1), :] = jnp.where(owner == k, source, jnp.zeros_like(source))
            weights = w_ref[n, :, rows * per_chunk * u : rows * per_chunk * (u + 1)]
            term = jnp.dot(weights, rhs_ref[...], preferred_element_type=jnp.float32)
            acc = acc + term.astype(jnp.bfloat16).astype(jnp.float32)
        o_ref[:, lanes] = (q_ref[:, lanes].astype(jnp.float32) * acc).astype(o_ref.dtype)


def shards(queries, keys, values, taps, segment_ids):
    rows = queries.shape[0]
    channels = queries.shape[1]
    filters = taps.shape[1]
    group_size = channels // filters
    ctx_count = lax.axis_size("ctx")
    own_index = lax.axis_index("ctx")
    core = own_index % 2
    tap_rows = taps.shape[0]
    filt_len = tap_rows * ctx_count
    lags = filt_len // rows
    seg_row = jnp.zeros((1, filters), jnp.bfloat16).at[0, :rows].set(segment_ids.astype(jnp.bfloat16))
    packed = jnp.concatenate([taps, seg_row], axis=0)
    packed = lax.all_gather(packed, "ctx", axis=0, tiled=False)
    packed, keys, values = lax.optimization_barrier((packed, keys, values))
    all_taps = packed[:, :tap_rows].reshape(filt_len, filters).astype(jnp.float32)
    all_segs = packed[:, tap_rows, :rows].astype(jnp.int32)
    gated = (keys.astype(jnp.float32) * values.astype(jnp.float32)).astype(jnp.bfloat16)
    padded = jnp.concatenate(
        [
            jnp.zeros((filters, rows + 1), jnp.float32),
            all_taps.T[:, ::-1],
            jnp.zeros((filters, rows - 1), jnp.float32),
        ],
        axis=1,
    )
    seg_sources = [
        lax.dynamic_index_in_dim(all_segs, jnp.maximum(own_index - lag, 0), 0, keepdims=False)
        for lag in range(lags, -1, -1)
    ]
    mask = (segment_ids[:, None] == jnp.concatenate(seg_sources)[None, :]).astype(jnp.float32)
    two_back = shifted(gated, "ctx", 2)
    four_back = shifted(gated, "ctx", 4)
    lane_chunk = 128
    step_lanes = lane_chunk * 4 if channels % (lane_chunk * 4) == 0 else lane_chunk
    span = (lags + 1) * rows
    step_filters = step_lanes // group_size
    weights, own_term = pl.pallas_call(
        functools.partial(weight_kernel, lags=lags, rows=rows, group_size=group_size),
        grid=(channels // step_lanes,),
        in_specs=[
            pl.BlockSpec((step_filters, (lags + 2) * rows), lambda j: (j, 0)),
            pl.BlockSpec((rows, span), lambda j: (0, 0)),
            pl.BlockSpec((rows, step_lanes), lambda j: (0, j)),
        ],
        out_specs=[
            pl.BlockSpec((lags, rows, step_filters * rows), lambda j: (0, 0, j)),
            pl.BlockSpec((rows, step_lanes), lambda j: (0, j)),
        ],
        out_shape=[
            jax.ShapeDtypeStruct((lags, rows, filters * rows), jnp.bfloat16),
            jax.ShapeDtypeStruct((rows, channels), jnp.float32),
        ],
        scratch_shapes=[
            pltpu.VMEM((rows, rows * (lane_chunk // group_size)), jnp.bfloat16),
            pltpu.VMEM((rows * (lane_chunk // group_size), lane_chunk), jnp.bfloat16),
        ],
    )(padded, mask, gated)
    weights, own_term, two_back, four_back = lax.optimization_barrier((weights, own_term, two_back, four_back))
    swap_a = swapped(two_back, "ctx")
    pairs = [(source, source ^ 1) for source in range(ctx_count)]
    sibling_own = lax.ppermute(gated, "ctx", [(s, d) for s, d in pairs if s % 2 == 0])
    sibling_four = lax.ppermute(four_back, "ctx", [(s, d) for s, d in pairs if s % 2 == 1])
    sources = [four_back, sibling_four, two_back, swap_a, sibling_own]
    kernel = functools.partial(conv_kernel, lags=lags, rows=rows, group_size=group_size)
    block = pl.BlockSpec((rows, step_lanes), lambda j, c: (0, j))
    return pl.pallas_call(
        kernel,
        grid_spec=pltpu.PrefetchScalarGridSpec(
            num_scalar_prefetch=1,
            grid=(channels // step_lanes,),
            in_specs=[block] * (lags + 1)
            + [
                pl.BlockSpec((lags, rows, step_filters * rows), lambda j, c: (0, 0, j)),
                block,
                block,
            ],
            out_specs=block,
            scratch_shapes=[pltpu.VMEM((rows * (lane_chunk // group_size), lane_chunk), jnp.bfloat16)],
        ),
        out_shape=jax.ShapeDtypeStruct((rows, channels), jnp.bfloat16),
    )(jnp.reshape(core, (1,)).astype(jnp.int32), *sources, weights, own_term, queries)


def solution(mesh):
    return jax.shard_map(
        shards,
        mesh=mesh,
        in_specs=(
            P(("dp", "ctx"), None),
            P(("dp", "ctx"), None),
            P(("dp", "ctx"), None),
            P("ctx", None),
            P(("dp", "ctx")),
        ),
        out_specs=P(("dp", "ctx"), None),
        check_vma=False,
    )
```

```python
import functools

import jax
import jax.numpy as jnp
from jax import lax
from jax.experimental import pallas as pl
from jax.experimental.pallas import tpu as pltpu
from jax.sharding import PartitionSpec as P


def shifted(value, axis, steps):
    count = lax.axis_size(axis)
    first, last = (max(0, -steps), min(count, count - steps))
    return lax.ppermute(value, axis, [(source, source + steps) for source in range(first, last)])


def swapped(value, axis):
    count = lax.axis_size(axis)
    return lax.ppermute(value, axis, [(source, source ^ 1) for source in range(count)])


def gathered(value, axis):
    count = lax.axis_size(axis)
    if count & (count - 1):
        return lax.all_gather(value, axis, axis=0, tiled=False)
    index = lax.axis_index(axis)
    blocks = value[None]
    step = 1
    while step < count:
        received = lax.ppermute(blocks, axis, [(s, s ^ step) for s in range(count)])
        later = (index & step) != 0
        blocks = jnp.where(later, jnp.concatenate([received, blocks]), jnp.concatenate([blocks, received]))
        step *= 2
    return blocks


def weight_kernel(p_ref, m_ref, g_ref, w_ref, a_ref, lhs_ref, rhs_ref, *, lags, rows, group_size):
    row = lax.broadcasted_iota(jnp.int32, (rows, rows), 0)
    upper = lax.broadcasted_iota(jnp.int32, (rows, rows), 1) >= row
    lane_chunk = rhs_ref.shape[1]
    per_chunk = lane_chunk // group_size
    owner = lax.broadcasted_iota(jnp.int32, (rows, lane_chunk), 1) // group_size
    for u in range(g_ref.shape[1] // lane_chunk):
        for j in range(per_chunk):
            k = u * per_chunk + j
            tap_row = p_ref[k : k + 1, :]
            rolled = [
                pltpu.roll(
                    jnp.broadcast_to(tap_row[:, rows * m : rows * (m + 1)], (rows, rows)),
                    0,
                    1,
                    stride=1,
                    stride_axis=0,
                )
                for m in range(lags + 2)
            ]
            for n in range(lags + 1):
                tile = jnp.where(upper, rolled[n + 1], rolled[n]) * m_ref[:, rows * n : rows * (n + 1)]
                if n < lags:
                    w_ref[n, :, rows * k : rows * (k + 1)] = tile.astype(jnp.bfloat16)
                else:
                    lhs_ref[:, rows * j : rows * (j + 1)] = tile.astype(jnp.bfloat16)
        lanes = slice(lane_chunk * u, lane_chunk * (u + 1))
        source = g_ref[:, lanes]
        for j in range(per_chunk):
            rhs_ref[rows * j : rows * (j + 1), :] = jnp.where(owner == j, source, jnp.zeros_like(source))
        a_ref[:, lanes] = jnp.dot(lhs_ref[...], rhs_ref[...], preferred_element_type=jnp.float32)


def conv_kernel(core_ref, *refs, lags, rows, group_size):
    g_refs = list(refs[:lags])
    w_ref, a_ref, q_ref, o_ref, rhs_ref = refs[lags:]
    lane_chunk = rhs_ref.shape[1]
    per_chunk = lane_chunk // group_size
    owner = lax.broadcasted_iota(jnp.int32, (rows, lane_chunk), 1) // group_size
    even = core_ref[0] == 0
    for u in range(q_ref.shape[1] // lane_chunk):
        lanes = slice(lane_chunk * u, lane_chunk * (u + 1))
        blocks = [g[:, lanes] for g in g_refs]
        near, far = blocks[lags - 1], blocks[lags - 3]
        blocks[lags - 1] = jnp.where(even, near, far)
        blocks[lags - 3] = jnp.where(even, far, near)
        acc = a_ref[:, lanes]
        for n in range(lags):
            source = blocks[n]
            for k in range(per_chunk):
                rhs_ref[rows * k : rows * (k + 1), :] = jnp.where(owner == k, source, jnp.zeros_like(source))
            weights = w_ref[n, :, rows * per_chunk * u : rows * per_chunk * (u + 1)]
            term = jnp.dot(weights, rhs_ref[...], preferred_element_type=jnp.float32)
            acc = acc + term.astype(jnp.bfloat16).astype(jnp.float32)
        o_ref[:, lanes] = (q_ref[:, lanes].astype(jnp.float32) * acc).astype(o_ref.dtype)


def shards(queries, keys, values, taps, segment_ids):
    rows = queries.shape[0]
    channels = queries.shape[1]
    filters = taps.shape[1]
    group_size = channels // filters
    ctx_count = lax.axis_size("ctx")
    own_index = lax.axis_index("ctx")
    core = own_index % 2
    tap_rows = taps.shape[0]
    filt_len = tap_rows * ctx_count
    lags = filt_len // rows
    seg_row = jnp.zeros((1, filters), jnp.bfloat16).at[0, :rows].set(segment_ids.astype(jnp.bfloat16))
    packed = jnp.concatenate([taps, seg_row], axis=0)
    packed = gathered(packed, "ctx")
    packed, keys, values = lax.optimization_barrier((packed, keys, values))
    all_taps = packed[:, :tap_rows].reshape(filt_len, filters).astype(jnp.float32)
    all_segs = packed[:, tap_rows, :rows].astype(jnp.int32)
    gated = (keys.astype(jnp.float32) * values.astype(jnp.float32)).astype(jnp.bfloat16)
    padded = jnp.concatenate(
        [
            jnp.zeros((filters, rows + 1), jnp.float32),
            all_taps.T[:, ::-1],
            jnp.zeros((filters, rows - 1), jnp.float32),
        ],
        axis=1,
    )
    seg_sources = [
        lax.dynamic_index_in_dim(all_segs, jnp.maximum(own_index - lag, 0), 0, keepdims=False)
        for lag in range(lags, -1, -1)
    ]
    mask = (segment_ids[:, None] == jnp.concatenate(seg_sources)[None, :]).astype(jnp.float32)
    two_back = shifted(gated, "ctx", 2)
    four_back = shifted(gated, "ctx", 4)
    lane_chunk = 128
    step_lanes = lane_chunk * 4 if channels % (lane_chunk * 4) == 0 else lane_chunk
    span = (lags + 1) * rows
    step_filters = step_lanes // group_size
    weights, own_term = pl.pallas_call(
        functools.partial(weight_kernel, lags=lags, rows=rows, group_size=group_size),
        grid=(channels // step_lanes,),
        in_specs=[
            pl.BlockSpec((step_filters, (lags + 2) * rows), lambda j: (j, 0)),
            pl.BlockSpec((rows, span), lambda j: (0, 0)),
            pl.BlockSpec((rows, step_lanes), lambda j: (0, j)),
        ],
        out_specs=[
            pl.BlockSpec((lags, rows, step_filters * rows), lambda j: (0, 0, j)),
            pl.BlockSpec((rows, step_lanes), lambda j: (0, j)),
        ],
        out_shape=[
            jax.ShapeDtypeStruct((lags, rows, filters * rows), jnp.bfloat16),
            jax.ShapeDtypeStruct((rows, channels), jnp.float32),
        ],
        scratch_shapes=[
            pltpu.VMEM((rows, rows * (lane_chunk // group_size)), jnp.bfloat16),
            pltpu.VMEM((rows * (lane_chunk // group_size), lane_chunk), jnp.bfloat16),
        ],
    )(padded, mask, gated)
    weights, own_term, two_back, four_back = lax.optimization_barrier((weights, own_term, two_back, four_back))
    swap_a = swapped(two_back, "ctx")
    swap_b = swapped(jnp.where(core == 1, four_back, gated), "ctx")
    sources = [four_back, swap_b, two_back, swap_a]
    kernel = functools.partial(conv_kernel, lags=lags, rows=rows, group_size=group_size)
    block = pl.BlockSpec((rows, step_lanes), lambda j, c: (0, j))
    return pl.pallas_call(
        kernel,
        grid_spec=pltpu.PrefetchScalarGridSpec(
            num_scalar_prefetch=1,
            grid=(channels // step_lanes,),
            in_specs=[block] * lags
            + [
                pl.BlockSpec((lags, rows, step_filters * rows), lambda j, c: (0, 0, j)),
                block,
                block,
            ],
            out_specs=block,
            scratch_shapes=[pltpu.VMEM((rows * (lane_chunk // group_size), lane_chunk), jnp.bfloat16)],
        ),
        out_shape=jax.ShapeDtypeStruct((rows, channels), jnp.bfloat16),
    )(jnp.reshape(core, (1,)).astype(jnp.int32), *sources, weights, own_term, queries)


def solution(mesh):
    return jax.shard_map(
        shards,
        mesh=mesh,
        in_specs=(
            P(("dp", "ctx"), None),
            P(("dp", "ctx"), None),
            P(("dp", "ctx"), None),
            P("ctx", None),
            P(("dp", "ctx")),
        ),
        out_specs=P(("dp", "ctx"), None),
        check_vma=False,
    )
```

```python
import functools

import jax
import jax.numpy as jnp
from jax import lax
from jax.experimental import pallas as pl
from jax.experimental.pallas import tpu as pltpu
from jax.sharding import PartitionSpec as P


def shifted(value, axis, steps):
    count = lax.axis_size(axis)
    first, last = (max(0, -steps), min(count, count - steps))
    return lax.ppermute(value, axis, [(source, source + steps) for source in range(first, last)])


def swapped(value, axis):
    count = lax.axis_size(axis)
    return lax.ppermute(value, axis, [(source, source ^ 1) for source in range(count)])


def gathered(value, axis):
    count = lax.axis_size(axis)
    if count & (count - 1):
        return lax.all_gather(value, axis, axis=0, tiled=False)
    index = lax.axis_index(axis)
    blocks = value[None]
    step = 1
    while step < count:
        received = lax.ppermute(blocks, axis, [(s, s ^ step) for s in range(count)])
        later = (index & step) != 0
        blocks = jnp.where(later, jnp.concatenate([received, blocks]), jnp.concatenate([blocks, received]))
        step *= 2
    return blocks


def weight_kernel(p_ref, m_ref, g_ref, w_ref, a_ref, lhs_ref, rhs_ref, *, lags, rows, group_size):
    row = lax.broadcasted_iota(jnp.int32, (rows, rows), 0)
    upper = lax.broadcasted_iota(jnp.int32, (rows, rows), 1) >= row
    lane_chunk = rhs_ref.shape[1]
    per_chunk = lane_chunk // group_size
    owner = lax.broadcasted_iota(jnp.int32, (rows, lane_chunk), 1) // group_size
    for u in range(g_ref.shape[1] // lane_chunk):
        for j in range(per_chunk):
            k = u * per_chunk + j
            tap_row = p_ref[k : k + 1, :]
            rolled = [
                pltpu.roll(
                    jnp.broadcast_to(tap_row[:, rows * m : rows * (m + 1)], (rows, rows)),
                    0,
                    1,
                    stride=1,
                    stride_axis=0,
                )
                for m in range(lags + 2)
            ]
            for n in range(lags + 1):
                tile = jnp.where(upper, rolled[n + 1], rolled[n]) * m_ref[:, rows * n : rows * (n + 1)]
                if n < lags:
                    w_ref[n, :, rows * k : rows * (k + 1)] = tile.astype(jnp.bfloat16)
                else:
                    lhs_ref[:, rows * j : rows * (j + 1)] = tile.astype(jnp.bfloat16)
        lanes = slice(lane_chunk * u, lane_chunk * (u + 1))
        source = g_ref[:, lanes]
        for j in range(per_chunk):
            rhs_ref[rows * j : rows * (j + 1), :] = jnp.where(owner == j, source, jnp.zeros_like(source))
        a_ref[:, lanes] = jnp.dot(lhs_ref[...], rhs_ref[...], preferred_element_type=jnp.float32)


def conv_kernel(core_ref, *refs, lags, rows, group_size):
    g_refs = list(refs[:lags])
    w_ref, a_ref, q_ref, o_ref, rhs_ref = refs[lags:]
    lane_chunk = rhs_ref.shape[1]
    per_chunk = lane_chunk // group_size
    owner = lax.broadcasted_iota(jnp.int32, (rows, lane_chunk), 1) // group_size
    even = core_ref[0] == 0
    for u in range(q_ref.shape[1] // lane_chunk):
        lanes = slice(lane_chunk * u, lane_chunk * (u + 1))
        blocks = [g[:, lanes] for g in g_refs]
        near, far = blocks[lags - 1], blocks[lags - 3]
        blocks[lags - 1] = jnp.where(even, near, far)
        blocks[lags - 3] = jnp.where(even, far, near)
        acc = a_ref[:, lanes]
        for n in range(lags):
            source = blocks[n]
            for k in range(per_chunk):
                rhs_ref[rows * k : rows * (k + 1), :] = jnp.where(owner == k, source, jnp.zeros_like(source))
            weights = w_ref[n, :, rows * per_chunk * u : rows * per_chunk * (u + 1)]
            term = jnp.dot(weights, rhs_ref[...], preferred_element_type=jnp.float32)
            acc = acc + term.astype(jnp.bfloat16).astype(jnp.float32)
        o_ref[:, lanes] = (q_ref[:, lanes].astype(jnp.float32) * acc).astype(o_ref.dtype)


def shards(queries, keys, values, taps, segment_ids):
    rows = queries.shape[0]
    channels = queries.shape[1]
    filters = taps.shape[1]
    group_size = channels // filters
    ctx_count = lax.axis_size("ctx")
    own_index = lax.axis_index("ctx")
    core = own_index % 2
    tap_rows = taps.shape[0]
    filt_len = tap_rows * ctx_count
    lags = filt_len // rows
    seg_row = jnp.zeros((1, filters), jnp.bfloat16).at[0, :rows].set(segment_ids.astype(jnp.bfloat16))
    packed = jnp.concatenate([taps, seg_row], axis=0)
    gated = (keys.astype(jnp.float32) * values.astype(jnp.float32)).astype(jnp.bfloat16)
    packed = gathered(packed, "ctx")
    packed, gated = lax.optimization_barrier((packed, gated))
    all_taps = packed[:, :tap_rows].reshape(filt_len, filters).astype(jnp.float32)
    all_segs = packed[:, tap_rows, :rows].astype(jnp.int32)
    padded = jnp.concatenate(
        [
            jnp.zeros((filters, rows + 1), jnp.float32),
            all_taps.T[:, ::-1],
            jnp.zeros((filters, rows - 1), jnp.float32),
        ],
        axis=1,
    )
    seg_sources = [
        lax.dynamic_index_in_dim(all_segs, jnp.maximum(own_index - lag, 0), 0, keepdims=False)
        for lag in range(lags, -1, -1)
    ]
    mask = (segment_ids[:, None] == jnp.concatenate(seg_sources)[None, :]).astype(jnp.float32)
    two_back = shifted(gated, "ctx", 2)
    four_back = shifted(gated, "ctx", 4)
    lane_chunk = 128
    step_lanes = lane_chunk * 4 if channels % (lane_chunk * 4) == 0 else lane_chunk
    span = (lags + 1) * rows
    step_filters = step_lanes // group_size
    weights, own_term = pl.pallas_call(
        functools.partial(weight_kernel, lags=lags, rows=rows, group_size=group_size),
        grid=(channels // step_lanes,),
        in_specs=[
            pl.BlockSpec((step_filters, (lags + 2) * rows), lambda j: (j, 0)),
            pl.BlockSpec((rows, span), lambda j: (0, 0)),
            pl.BlockSpec((rows, step_lanes), lambda j: (0, j)),
        ],
        out_specs=[
            pl.BlockSpec((lags, rows, step_filters * rows), lambda j: (0, 0, j)),
            pl.BlockSpec((rows, step_lanes), lambda j: (0, j)),
        ],
        out_shape=[
            jax.ShapeDtypeStruct((lags, rows, filters * rows), jnp.bfloat16),
            jax.ShapeDtypeStruct((rows, channels), jnp.float32),
        ],
        scratch_shapes=[
            pltpu.VMEM((rows, rows * (lane_chunk // group_size)), jnp.bfloat16),
            pltpu.VMEM((rows * (lane_chunk // group_size), lane_chunk), jnp.bfloat16),
        ],
    )(padded, mask, gated)
    weights, own_term, two_back, four_back = lax.optimization_barrier((weights, own_term, two_back, four_back))
    swap_a = swapped(two_back, "ctx")
    swap_b = swapped(jnp.where(core == 1, four_back, gated), "ctx")
    sources = [four_back, swap_b, two_back, swap_a]
    kernel = functools.partial(conv_kernel, lags=lags, rows=rows, group_size=group_size)
    block = pl.BlockSpec((rows, step_lanes), lambda j, c: (0, j))
    return pl.pallas_call(
        kernel,
        grid_spec=pltpu.PrefetchScalarGridSpec(
            num_scalar_prefetch=1,
            grid=(channels // step_lanes,),
            in_specs=[block] * lags
            + [
                pl.BlockSpec((lags, rows, step_filters * rows), lambda j, c: (0, 0, j)),
                block,
                block,
            ],
            out_specs=block,
            scratch_shapes=[pltpu.VMEM((rows * (lane_chunk // group_size), lane_chunk), jnp.bfloat16)],
        ),
        out_shape=jax.ShapeDtypeStruct((rows, channels), jnp.bfloat16),
    )(jnp.reshape(core, (1,)).astype(jnp.int32), *sources, weights, own_term, queries)


def solution(mesh):
    return jax.shard_map(
        shards,
        mesh=mesh,
        in_specs=(
            P(("dp", "ctx"), None),
            P(("dp", "ctx"), None),
            P(("dp", "ctx"), None),
            P("ctx", None),
            P(("dp", "ctx")),
        ),
        out_specs=P(("dp", "ctx"), None),
        check_vma=False,
    )
```

```python
import functools

import jax
import jax.numpy as jnp
from jax import lax
from jax.experimental import pallas as pl
from jax.experimental.pallas import tpu as pltpu
from jax.sharding import PartitionSpec as P


def shifted(value, axis, steps):
    count = lax.axis_size(axis)
    first, last = (max(0, -steps), min(count, count - steps))
    return lax.ppermute(value, axis, [(source, source + steps) for source in range(first, last)])


def swapped(value, axis):
    count = lax.axis_size(axis)
    return lax.ppermute(value, axis, [(source, source ^ 1) for source in range(count)])


def gathered(value, axis):
    count = lax.axis_size(axis)
    if count & (count - 1):
        return lax.all_gather(value, axis, axis=0, tiled=False)
    index = lax.axis_index(axis)
    blocks = value[None]
    step = count // 2
    while step >= 1:
        received = lax.ppermute(blocks, axis, [(s, s ^ step) for s in range(count)])
        later = (index & step) != 0
        blocks = jnp.where(later, jnp.concatenate([received, blocks]), jnp.concatenate([blocks, received]))
        step //= 2
    rounds = count.bit_length() - 1
    blocks = blocks.reshape((2,) * rounds + value.shape)
    blocks = blocks.transpose(tuple(range(rounds))[::-1] + tuple(range(rounds, rounds + value.ndim)))
    return blocks.reshape((count,) + value.shape)


def weight_kernel(p_ref, m_ref, g_ref, w_ref, a_ref, lhs_ref, rhs_ref, *, lags, rows, group_size):
    row = lax.broadcasted_iota(jnp.int32, (rows, rows), 0)
    upper = lax.broadcasted_iota(jnp.int32, (rows, rows), 1) >= row
    lane_chunk = rhs_ref.shape[1]
    per_chunk = lane_chunk // group_size
    owner = lax.broadcasted_iota(jnp.int32, (rows, lane_chunk), 1) // group_size
    for u in range(g_ref.shape[1] // lane_chunk):
        for j in range(per_chunk):
            k = u * per_chunk + j
            tap_row = p_ref[k : k + 1, :]
            rolled = [
                pltpu.roll(
                    jnp.broadcast_to(tap_row[:, rows * m : rows * (m + 1)], (rows, rows)),
                    0,
                    1,
                    stride=1,
                    stride_axis=0,
                )
                for m in range(lags + 2)
            ]
            for n in range(lags + 1):
                tile = jnp.where(upper, rolled[n + 1], rolled[n]) * m_ref[:, rows * n : rows * (n + 1)]
                if n < lags:
                    w_ref[n, :, rows * k : rows * (k + 1)] = tile.astype(jnp.bfloat16)
                else:
                    lhs_ref[:, rows * j : rows * (j + 1)] = tile.astype(jnp.bfloat16)
        lanes = slice(lane_chunk * u, lane_chunk * (u + 1))
        source = g_ref[:, lanes]
        for j in range(per_chunk):
            rhs_ref[rows * j : rows * (j + 1), :] = jnp.where(owner == j, source, jnp.zeros_like(source))
        a_ref[:, lanes] = jnp.dot(lhs_ref[...], rhs_ref[...], preferred_element_type=jnp.float32)


def conv_kernel(core_ref, *refs, lags, rows, group_size):
    g_refs = list(refs[:lags])
    w_ref, a_ref, q_ref, o_ref, rhs_ref = refs[lags:]
    lane_chunk = rhs_ref.shape[1]
    per_chunk = lane_chunk // group_size
    owner = lax.broadcasted_iota(jnp.int32, (rows, lane_chunk), 1) // group_size
    even = core_ref[0] == 0
    for u in range(q_ref.shape[1] // lane_chunk):
        lanes = slice(lane_chunk * u, lane_chunk * (u + 1))
        blocks = [g[:, lanes] for g in g_refs]
        near, far = blocks[lags - 1], blocks[lags - 3]
        blocks[lags - 1] = jnp.where(even, near, far)
        blocks[lags - 3] = jnp.where(even, far, near)
        acc = a_ref[:, lanes]
        for n in range(lags):
            source = blocks[n]
            for k in range(per_chunk):
                rhs_ref[rows * k : rows * (k + 1), :] = jnp.where(owner == k, source, jnp.zeros_like(source))
            weights = w_ref[n, :, rows * per_chunk * u : rows * per_chunk * (u + 1)]
            term = jnp.dot(weights, rhs_ref[...], preferred_element_type=jnp.float32)
            acc = acc + term.astype(jnp.bfloat16).astype(jnp.float32)
        o_ref[:, lanes] = (q_ref[:, lanes].astype(jnp.float32) * acc).astype(o_ref.dtype)


def shards(queries, keys, values, taps, segment_ids):
    rows = queries.shape[0]
    channels = queries.shape[1]
    filters = taps.shape[1]
    group_size = channels // filters
    ctx_count = lax.axis_size("ctx")
    own_index = lax.axis_index("ctx")
    core = own_index % 2
    tap_rows = taps.shape[0]
    filt_len = tap_rows * ctx_count
    lags = filt_len // rows
    seg_row = jnp.zeros((1, filters), jnp.bfloat16).at[0, :rows].set(segment_ids.astype(jnp.bfloat16))
    packed = jnp.concatenate([taps, seg_row], axis=0)
    gated = (keys.astype(jnp.float32) * values.astype(jnp.float32)).astype(jnp.bfloat16)
    packed = gathered(packed, "ctx")
    packed, gated = lax.optimization_barrier((packed, gated))
    all_taps = packed[:, :tap_rows].reshape(filt_len, filters).astype(jnp.float32)
    all_segs = packed[:, tap_rows, :rows].astype(jnp.int32)
    padded = jnp.concatenate(
        [
            jnp.zeros((filters, rows + 1), jnp.float32),
            all_taps.T[:, ::-1],
            jnp.zeros((filters, rows - 1), jnp.float32),
        ],
        axis=1,
    )
    seg_sources = [
        lax.dynamic_index_in_dim(all_segs, jnp.maximum(own_index - lag, 0), 0, keepdims=False)
        for lag in range(lags, -1, -1)
    ]
    mask = (segment_ids[:, None] == jnp.concatenate(seg_sources)[None, :]).astype(jnp.float32)
    two_back = shifted(gated, "ctx", 2)
    four_back = shifted(gated, "ctx", 4)
    lane_chunk = 128
    step_lanes = lane_chunk * 4 if channels % (lane_chunk * 4) == 0 else lane_chunk
    span = (lags + 1) * rows
    step_filters = step_lanes // group_size
    weights, own_term = pl.pallas_call(
        functools.partial(weight_kernel, lags=lags, rows=rows, group_size=group_size),
        grid=(channels // step_lanes,),
        in_specs=[
            pl.BlockSpec((step_filters, (lags + 2) * rows), lambda j: (j, 0)),
            pl.BlockSpec((rows, span), lambda j: (0, 0)),
            pl.BlockSpec((rows, step_lanes), lambda j: (0, j)),
        ],
        out_specs=[
            pl.BlockSpec((lags, rows, step_filters * rows), lambda j: (0, 0, j)),
            pl.BlockSpec((rows, step_lanes), lambda j: (0, j)),
        ],
        out_shape=[
            jax.ShapeDtypeStruct((lags, rows, filters * rows), jnp.bfloat16),
            jax.ShapeDtypeStruct((rows, channels), jnp.float32),
        ],
        scratch_shapes=[
            pltpu.VMEM((rows, rows * (lane_chunk // group_size)), jnp.bfloat16),
            pltpu.VMEM((rows * (lane_chunk // group_size), lane_chunk), jnp.bfloat16),
        ],
    )(padded, mask, gated)
    weights, own_term, two_back, four_back = lax.optimization_barrier((weights, own_term, two_back, four_back))
    swap_a = swapped(two_back, "ctx")
    swap_b = swapped(jnp.where(core == 1, four_back, gated), "ctx")
    sources = [four_back, swap_b, two_back, swap_a]
    kernel = functools.partial(conv_kernel, lags=lags, rows=rows, group_size=group_size)
    block = pl.BlockSpec((rows, step_lanes), lambda j, c: (0, j))
    return pl.pallas_call(
        kernel,
        grid_spec=pltpu.PrefetchScalarGridSpec(
            num_scalar_prefetch=1,
            grid=(channels // step_lanes,),
            in_specs=[block] * lags
            + [
                pl.BlockSpec((lags, rows, step_filters * rows), lambda j, c: (0, 0, j)),
                block,
                block,
            ],
            out_specs=block,
            scratch_shapes=[pltpu.VMEM((rows * (lane_chunk // group_size), lane_chunk), jnp.bfloat16)],
        ),
        out_shape=jax.ShapeDtypeStruct((rows, channels), jnp.bfloat16),
    )(jnp.reshape(core, (1,)).astype(jnp.int32), *sources, weights, own_term, queries)


def solution(mesh):
    return jax.shard_map(
        shards,
        mesh=mesh,
        in_specs=(
            P(("dp", "ctx"), None),
            P(("dp", "ctx"), None),
            P(("dp", "ctx"), None),
            P("ctx", None),
            P(("dp", "ctx")),
        ),
        out_specs=P(("dp", "ctx"), None),
        check_vma=False,
    )
```

```python
import functools

import jax
import jax.numpy as jnp
from jax import lax
from jax.experimental import pallas as pl
from jax.experimental.pallas import tpu as pltpu
from jax.sharding import PartitionSpec as P


def shifted(value, axis, steps):
    count = lax.axis_size(axis)
    first, last = (max(0, -steps), min(count, count - steps))
    return lax.ppermute(value, axis, [(source, source + steps) for source in range(first, last)])


def swapped(value, axis):
    count = lax.axis_size(axis)
    return lax.ppermute(value, axis, [(source, source ^ 1) for source in range(count)])


def gather_rounds(blocks, axis, steps):
    index = lax.axis_index(axis)
    count = lax.axis_size(axis)
    for step in steps:
        received = lax.ppermute(blocks, axis, [(s, s ^ step) for s in range(count)])
        later = (index & step) != 0
        blocks = jnp.where(later, jnp.concatenate([received, blocks]), jnp.concatenate([blocks, received]))
    return blocks


def unreversed(blocks, count):
    rounds = count.bit_length() - 1
    shape = blocks.shape[1:]
    blocks = blocks.reshape((2,) * rounds + shape)
    blocks = blocks.transpose(tuple(range(rounds))[::-1] + tuple(range(rounds, rounds + len(shape))))
    return blocks.reshape((count,) + shape)


def weight_kernel(p_ref, m_ref, g_ref, w_ref, a_ref, lhs_ref, rhs_ref, *, lags, rows, group_size):
    row = lax.broadcasted_iota(jnp.int32, (rows, rows), 0)
    upper = lax.broadcasted_iota(jnp.int32, (rows, rows), 1) >= row
    lane_chunk = rhs_ref.shape[1]
    per_chunk = lane_chunk // group_size
    owner = lax.broadcasted_iota(jnp.int32, (rows, lane_chunk), 1) // group_size
    for u in range(g_ref.shape[1] // lane_chunk):
        for j in range(per_chunk):
            k = u * per_chunk + j
            tap_row = p_ref[k : k + 1, :]
            rolled = [
                pltpu.roll(
                    jnp.broadcast_to(tap_row[:, rows * m : rows * (m + 1)], (rows, rows)),
                    0,
                    1,
                    stride=1,
                    stride_axis=0,
                )
                for m in range(lags + 2)
            ]
            for n in range(lags + 1):
                tile = jnp.where(upper, rolled[n + 1], rolled[n]) * m_ref[:, rows * n : rows * (n + 1)]
                if n < lags:
                    w_ref[n, :, rows * k : rows * (k + 1)] = tile.astype(jnp.bfloat16)
                else:
                    lhs_ref[:, rows * j : rows * (j + 1)] = tile.astype(jnp.bfloat16)
        lanes = slice(lane_chunk * u, lane_chunk * (u + 1))
        source = g_ref[:, lanes]
        for j in range(per_chunk):
            rhs_ref[rows * j : rows * (j + 1), :] = jnp.where(owner == j, source, jnp.zeros_like(source))
        a_ref[:, lanes] = jnp.dot(lhs_ref[...], rhs_ref[...], preferred_element_type=jnp.float32)


def conv_kernel(core_ref, *refs, lags, rows, group_size):
    g_refs = list(refs[:lags])
    w_ref, a_ref, q_ref, o_ref, rhs_ref = refs[lags:]
    lane_chunk = rhs_ref.shape[1]
    per_chunk = lane_chunk // group_size
    owner = lax.broadcasted_iota(jnp.int32, (rows, lane_chunk), 1) // group_size
    even = core_ref[0] == 0
    for u in range(q_ref.shape[1] // lane_chunk):
        lanes = slice(lane_chunk * u, lane_chunk * (u + 1))
        blocks = [g[:, lanes] for g in g_refs]
        near, far = blocks[lags - 1], blocks[lags - 3]
        blocks[lags - 1] = jnp.where(even, near, far)
        blocks[lags - 3] = jnp.where(even, far, near)
        acc = a_ref[:, lanes]
        for n in range(lags):
            source = blocks[n]
            for k in range(per_chunk):
                rhs_ref[rows * k : rows * (k + 1), :] = jnp.where(owner == k, source, jnp.zeros_like(source))
            weights = w_ref[n, :, rows * per_chunk * u : rows * per_chunk * (u + 1)]
            term = jnp.dot(weights, rhs_ref[...], preferred_element_type=jnp.float32)
            acc = acc + term.astype(jnp.bfloat16).astype(jnp.float32)
        o_ref[:, lanes] = (q_ref[:, lanes].astype(jnp.float32) * acc).astype(o_ref.dtype)


def shards(queries, keys, values, taps, segment_ids):
    rows = queries.shape[0]
    channels = queries.shape[1]
    filters = taps.shape[1]
    group_size = channels // filters
    ctx_count = lax.axis_size("ctx")
    own_index = lax.axis_index("ctx")
    core = own_index % 2
    tap_rows = taps.shape[0]
    filt_len = tap_rows * ctx_count
    lags = filt_len // rows
    seg_row = jnp.zeros((1, filters), jnp.bfloat16).at[0, :rows].set(segment_ids.astype(jnp.bfloat16))
    packed = jnp.concatenate([taps, seg_row], axis=0)
    gated = (keys.astype(jnp.float32) * values.astype(jnp.float32)).astype(jnp.bfloat16)
    assert ctx_count & (ctx_count - 1) == 0
    steps = [ctx_count >> r for r in range(1, ctx_count.bit_length())]
    packed = gather_rounds(packed[None], "ctx", steps[:-1])
    packed, gated = lax.optimization_barrier((packed, gated))
    two_back = shifted(gated, "ctx", 2)
    four_back = shifted(gated, "ctx", 4)
    packed = unreversed(gather_rounds(packed, "ctx", steps[-1:]), ctx_count)
    all_taps = packed[:, :tap_rows].reshape(filt_len, filters).astype(jnp.float32)
    all_segs = packed[:, tap_rows, :rows].astype(jnp.int32)
    padded = jnp.concatenate(
        [
            jnp.zeros((filters, rows + 1), jnp.float32),
            all_taps.T[:, ::-1],
            jnp.zeros((filters, rows - 1), jnp.float32),
        ],
        axis=1,
    )
    seg_sources = [
        lax.dynamic_index_in_dim(all_segs, jnp.maximum(own_index - lag, 0), 0, keepdims=False)
        for lag in range(lags, -1, -1)
    ]
    mask = (segment_ids[:, None] == jnp.concatenate(seg_sources)[None, :]).astype(jnp.float32)
    lane_chunk = 128
    step_lanes = lane_chunk * 4 if channels % (lane_chunk * 4) == 0 else lane_chunk
    span = (lags + 1) * rows
    step_filters = step_lanes // group_size
    weights, own_term = pl.pallas_call(
        functools.partial(weight_kernel, lags=lags, rows=rows, group_size=group_size),
        grid=(channels // step_lanes,),
        in_specs=[
            pl.BlockSpec((step_filters, (lags + 2) * rows), lambda j: (j, 0)),
            pl.BlockSpec((rows, span), lambda j: (0, 0)),
            pl.BlockSpec((rows, step_lanes), lambda j: (0, j)),
        ],
        out_specs=[
            pl.BlockSpec((lags, rows, step_filters * rows), lambda j: (0, 0, j)),
            pl.BlockSpec((rows, step_lanes), lambda j: (0, j)),
        ],
        out_shape=[
            jax.ShapeDtypeStruct((lags, rows, filters * rows), jnp.bfloat16),
            jax.ShapeDtypeStruct((rows, channels), jnp.float32),
        ],
        scratch_shapes=[
            pltpu.VMEM((rows, rows * (lane_chunk // group_size)), jnp.bfloat16),
            pltpu.VMEM((rows * (lane_chunk // group_size), lane_chunk), jnp.bfloat16),
        ],
    )(padded, mask, gated)
    weights, own_term, two_back, four_back = lax.optimization_barrier((weights, own_term, two_back, four_back))
    swap_a = swapped(two_back, "ctx")
    swap_b = swapped(jnp.where(core == 1, four_back, gated), "ctx")
    sources = [four_back, swap_b, two_back, swap_a]
    kernel = functools.partial(conv_kernel, lags=lags, rows=rows, group_size=group_size)
    block = pl.BlockSpec((rows, step_lanes), lambda j, c: (0, j))
    return pl.pallas_call(
        kernel,
        grid_spec=pltpu.PrefetchScalarGridSpec(
            num_scalar_prefetch=1,
            grid=(channels // step_lanes,),
            in_specs=[block] * lags
            + [
                pl.BlockSpec((lags, rows, step_filters * rows), lambda j, c: (0, 0, j)),
                block,
                block,
            ],
            out_specs=block,
            scratch_shapes=[pltpu.VMEM((rows * (lane_chunk // group_size), lane_chunk), jnp.bfloat16)],
        ),
        out_shape=jax.ShapeDtypeStruct((rows, channels), jnp.bfloat16),
    )(jnp.reshape(core, (1,)).astype(jnp.int32), *sources, weights, own_term, queries)


def solution(mesh):
    return jax.shard_map(
        shards,
        mesh=mesh,
        in_specs=(
            P(("dp", "ctx"), None),
            P(("dp", "ctx"), None),
            P(("dp", "ctx"), None),
            P("ctx", None),
            P(("dp", "ctx")),
        ),
        out_specs=P(("dp", "ctx"), None),
        check_vma=False,
    )
```

```python
import functools

import jax
import jax.numpy as jnp
from jax import lax
from jax.experimental import pallas as pl
from jax.experimental.pallas import tpu as pltpu
from jax.sharding import PartitionSpec as P


def shifted(value, axis, steps):
    count = lax.axis_size(axis)
    first, last = (max(0, -steps), min(count, count - steps))
    return lax.ppermute(value, axis, [(source, source + steps) for source in range(first, last)])


def swapped(value, axis):
    count = lax.axis_size(axis)
    return lax.ppermute(value, axis, [(source, source ^ 1) for source in range(count)])


def gather_rounds(blocks, axis, steps):
    index = lax.axis_index(axis)
    count = lax.axis_size(axis)
    for step in steps:
        received = lax.ppermute(blocks, axis, [(s, s ^ step) for s in range(count)])
        later = (index & step) != 0
        blocks = jnp.where(later, jnp.concatenate([received, blocks]), jnp.concatenate([blocks, received]))
    return blocks


def unreversed(blocks, count):
    rounds = count.bit_length() - 1
    shape = blocks.shape[1:]
    blocks = blocks.reshape((2,) * rounds + shape)
    blocks = blocks.transpose(tuple(range(rounds))[::-1] + tuple(range(rounds, rounds + len(shape))))
    return blocks.reshape((count,) + shape)


def weight_kernel(p_ref, m_ref, g_ref, w_ref, a_ref, lhs_ref, rhs_ref, *, lags, rows, group_size):
    row = lax.broadcasted_iota(jnp.int32, (rows, rows), 0)
    upper = lax.broadcasted_iota(jnp.int32, (rows, rows), 1) >= row
    lane_chunk = rhs_ref.shape[1]
    per_chunk = lane_chunk // group_size
    owner = lax.broadcasted_iota(jnp.int32, (rows, lane_chunk), 1) // group_size
    for u in range(g_ref.shape[1] // lane_chunk):
        for j in range(per_chunk):
            k = u * per_chunk + j
            tap_row = p_ref[k : k + 1, :]
            rolled = [
                pltpu.roll(
                    jnp.broadcast_to(tap_row[:, rows * m : rows * (m + 1)], (rows, rows)),
                    0,
                    1,
                    stride=1,
                    stride_axis=0,
                )
                for m in range(lags + 2)
            ]
            for n in range(lags + 1):
                tile = jnp.where(upper, rolled[n + 1], rolled[n]) * m_ref[:, rows * n : rows * (n + 1)]
                if n < lags:
                    w_ref[n, :, rows * k : rows * (k + 1)] = tile.astype(jnp.bfloat16)
                else:
                    lhs_ref[:, rows * j : rows * (j + 1)] = tile.astype(jnp.bfloat16)
        lanes = slice(lane_chunk * u, lane_chunk * (u + 1))
        source = g_ref[:, lanes]
        for j in range(per_chunk):
            rhs_ref[rows * j : rows * (j + 1), :] = jnp.where(owner == j, source, jnp.zeros_like(source))
        a_ref[:, lanes] = jnp.dot(lhs_ref[...], rhs_ref[...], preferred_element_type=jnp.float32)


def conv_kernel(core_ref, *refs, lags, rows, group_size):
    g_refs = list(refs[:lags])
    own_ref, w_ref, a_ref, q_ref, o_ref, rhs_ref = refs[lags:]
    lane_chunk = rhs_ref.shape[1]
    per_chunk = lane_chunk // group_size
    owner = lax.broadcasted_iota(jnp.int32, (rows, lane_chunk), 1) // group_size
    even = core_ref[0] == 0
    for u in range(q_ref.shape[1] // lane_chunk):
        lanes = slice(lane_chunk * u, lane_chunk * (u + 1))
        blocks = [g[:, lanes] for g in g_refs]
        blocks[lags - 3] = jnp.where(even, blocks[lags - 3], own_ref[:, lanes])
        near, far = blocks[lags - 1], blocks[lags - 3]
        blocks[lags - 1] = jnp.where(even, near, far)
        blocks[lags - 3] = jnp.where(even, far, near)
        acc = a_ref[:, lanes]
        for n in range(lags):
            source = blocks[n]
            for k in range(per_chunk):
                rhs_ref[rows * k : rows * (k + 1), :] = jnp.where(owner == k, source, jnp.zeros_like(source))
            weights = w_ref[n, :, rows * per_chunk * u : rows * per_chunk * (u + 1)]
            term = jnp.dot(weights, rhs_ref[...], preferred_element_type=jnp.float32)
            acc = acc + term.astype(jnp.bfloat16).astype(jnp.float32)
        o_ref[:, lanes] = (q_ref[:, lanes].astype(jnp.float32) * acc).astype(o_ref.dtype)


def shards(queries, keys, values, taps, segment_ids):
    rows = queries.shape[0]
    channels = queries.shape[1]
    filters = taps.shape[1]
    group_size = channels // filters
    ctx_count = lax.axis_size("ctx")
    own_index = lax.axis_index("ctx")
    core = own_index % 2
    tap_rows = taps.shape[0]
    filt_len = tap_rows * ctx_count
    lags = filt_len // rows
    seg_row = jnp.zeros((1, filters), jnp.bfloat16).at[0, :rows].set(segment_ids.astype(jnp.bfloat16))
    packed = jnp.concatenate([taps, seg_row], axis=0)
    gated = (keys.astype(jnp.float32) * values.astype(jnp.float32)).astype(jnp.bfloat16)
    assert ctx_count & (ctx_count - 1) == 0
    steps = [ctx_count >> r for r in range(1, ctx_count.bit_length())]
    packed = gather_rounds(packed[None], "ctx", steps[:-1])
    packed, gated = lax.optimization_barrier((packed, gated))
    two_back = shifted(gated, "ctx", 2)
    four_back = shifted(gated, "ctx", 4)
    packed = unreversed(gather_rounds(packed, "ctx", steps[-1:]), ctx_count)
    all_taps = packed[:, :tap_rows].reshape(filt_len, filters).astype(jnp.float32)
    all_segs = packed[:, tap_rows, :rows].astype(jnp.int32)
    padded = jnp.concatenate(
        [
            jnp.zeros((filters, rows + 1), jnp.float32),
            all_taps.T[:, ::-1],
            jnp.zeros((filters, rows - 1), jnp.float32),
        ],
        axis=1,
    )
    seg_sources = [
        lax.dynamic_index_in_dim(all_segs, jnp.maximum(own_index - lag, 0), 0, keepdims=False)
        for lag in range(lags, -1, -1)
    ]
    mask = (segment_ids[:, None] == jnp.concatenate(seg_sources)[None, :]).astype(jnp.float32)
    lane_chunk = 128
    step_lanes = lane_chunk * 4 if channels % (lane_chunk * 4) == 0 else lane_chunk
    span = (lags + 1) * rows
    step_filters = step_lanes // group_size
    weights, own_term = pl.pallas_call(
        functools.partial(weight_kernel, lags=lags, rows=rows, group_size=group_size),
        grid=(channels // step_lanes,),
        in_specs=[
            pl.BlockSpec((step_filters, (lags + 2) * rows), lambda j: (j, 0)),
            pl.BlockSpec((rows, span), lambda j: (0, 0)),
            pl.BlockSpec((rows, step_lanes), lambda j: (0, j)),
        ],
        out_specs=[
            pl.BlockSpec((lags, rows, step_filters * rows), lambda j: (0, 0, j)),
            pl.BlockSpec((rows, step_lanes), lambda j: (0, j)),
        ],
        out_shape=[
            jax.ShapeDtypeStruct((lags, rows, filters * rows), jnp.bfloat16),
            jax.ShapeDtypeStruct((rows, channels), jnp.float32),
        ],
        scratch_shapes=[
            pltpu.VMEM((rows, rows * (lane_chunk // group_size)), jnp.bfloat16),
            pltpu.VMEM((rows * (lane_chunk // group_size), lane_chunk), jnp.bfloat16),
        ],
    )(padded, mask, gated)
    weights, own_term, two_back, four_back = lax.optimization_barrier((weights, own_term, two_back, four_back))
    swap_a = swapped(two_back, "ctx")
    own_out, _ = lax.optimization_barrier((gated, packed))
    pairs = [(source, source ^ 1) for source in range(ctx_count)]
    sibling_own = lax.ppermute(own_out, "ctx", [(s, d) for s, d in pairs if s % 2 == 0])
    sibling_four = lax.ppermute(four_back, "ctx", [(s, d) for s, d in pairs if s % 2 == 1])
    sources = [four_back, sibling_four, two_back, swap_a, sibling_own]
    kernel = functools.partial(conv_kernel, lags=lags, rows=rows, group_size=group_size)
    block = pl.BlockSpec((rows, step_lanes), lambda j, c: (0, j))
    return pl.pallas_call(
        kernel,
        grid_spec=pltpu.PrefetchScalarGridSpec(
            num_scalar_prefetch=1,
            grid=(channels // step_lanes,),
            in_specs=[block] * (lags + 1)
            + [
                pl.BlockSpec((lags, rows, step_filters * rows), lambda j, c: (0, 0, j)),
                block,
                block,
            ],
            out_specs=block,
            scratch_shapes=[pltpu.VMEM((rows * (lane_chunk // group_size), lane_chunk), jnp.bfloat16)],
        ),
        out_shape=jax.ShapeDtypeStruct((rows, channels), jnp.bfloat16),
    )(jnp.reshape(core, (1,)).astype(jnp.int32), *sources, weights, own_term, queries)


def solution(mesh):
    return jax.shard_map(
        shards,
        mesh=mesh,
        in_specs=(
            P(("dp", "ctx"), None),
            P(("dp", "ctx"), None),
            P(("dp", "ctx"), None),
            P("ctx", None),
            P(("dp", "ctx")),
        ),
        out_specs=P(("dp", "ctx"), None),
        check_vma=False,
    )
```

```python
import functools

import jax
import jax.numpy as jnp
from jax import lax
from jax.experimental import pallas as pl
from jax.experimental.pallas import tpu as pltpu
from jax.sharding import PartitionSpec as P


def shifted(value, axis, steps):
    count = lax.axis_size(axis)
    first, last = (max(0, -steps), min(count, count - steps))
    return lax.ppermute(value, axis, [(source, source + steps) for source in range(first, last)])


def swapped(value, axis):
    count = lax.axis_size(axis)
    return lax.ppermute(value, axis, [(source, source ^ 1) for source in range(count)])


def gather_rounds(blocks, axis, steps):
    index = lax.axis_index(axis)
    count = lax.axis_size(axis)
    for step in steps:
        received = lax.ppermute(blocks, axis, [(s, s ^ step) for s in range(count)])
        later = (index & step) != 0
        blocks = jnp.where(later, jnp.concatenate([received, blocks]), jnp.concatenate([blocks, received]))
    return blocks


def unreversed(blocks, count):
    rounds = count.bit_length() - 1
    shape = blocks.shape[1:]
    blocks = blocks.reshape((2,) * rounds + shape)
    blocks = blocks.transpose(tuple(range(rounds))[::-1] + tuple(range(rounds, rounds + len(shape))))
    return blocks.reshape((count,) + shape)


def weight_kernel(p_ref, m_ref, g_ref, w_ref, a_ref, lhs_ref, rhs_ref, *, lags, rows, group_size):
    row = lax.broadcasted_iota(jnp.int32, (rows, rows), 0)
    upper = lax.broadcasted_iota(jnp.int32, (rows, rows), 1) >= row
    lane_chunk = rhs_ref.shape[1]
    per_chunk = lane_chunk // group_size
    owner = lax.broadcasted_iota(jnp.int32, (rows, lane_chunk), 1) // group_size
    for u in range(g_ref.shape[1] // lane_chunk):
        for j in range(per_chunk):
            k = u * per_chunk + j
            tap_row = p_ref[k : k + 1, :]
            rolled = [
                pltpu.roll(
                    jnp.broadcast_to(tap_row[:, rows * m : rows * (m + 1)], (rows, rows)),
                    0,
                    1,
                    stride=1,
                    stride_axis=0,
                )
                for m in range(lags + 2)
            ]
            for n in range(lags + 1):
                tile = jnp.where(upper, rolled[n + 1], rolled[n]) * m_ref[:, rows * n : rows * (n + 1)]
                if n < lags:
                    w_ref[n, :, rows * k : rows * (k + 1)] = tile.astype(jnp.bfloat16)
                else:
                    lhs_ref[:, rows * j : rows * (j + 1)] = tile.astype(jnp.bfloat16)
        lanes = slice(lane_chunk * u, lane_chunk * (u + 1))
        source = g_ref[:, lanes]
        for j in range(per_chunk):
            rhs_ref[rows * j : rows * (j + 1), :] = jnp.where(owner == j, source, jnp.zeros_like(source))
        a_ref[:, lanes] = jnp.dot(lhs_ref[...], rhs_ref[...], preferred_element_type=jnp.float32)


def conv_kernel(core_ref, *refs, lags, rows, group_size):
    g_refs = list(refs[:lags])
    own_ref, w_ref, a_ref, q_ref, o_ref, rhs_ref = refs[lags:]
    lane_chunk = rhs_ref.shape[1]
    per_chunk = lane_chunk // group_size
    owner = lax.broadcasted_iota(jnp.int32, (rows, lane_chunk), 1) // group_size
    even = core_ref[0] == 0
    for u in range(q_ref.shape[1] // lane_chunk):
        lanes = slice(lane_chunk * u, lane_chunk * (u + 1))
        blocks = [g[:, lanes] for g in g_refs]
        blocks[lags - 3] = jnp.where(even, blocks[lags - 3], own_ref[:, lanes])
        near, far = blocks[lags - 1], blocks[lags - 3]
        blocks[lags - 1] = jnp.where(even, near, far)
        blocks[lags - 3] = jnp.where(even, far, near)
        acc = a_ref[:, lanes]
        for n in range(lags):
            source = blocks[n]
            for k in range(per_chunk):
                rhs_ref[rows * k : rows * (k + 1), :] = jnp.where(owner == k, source, jnp.zeros_like(source))
            weights = w_ref[n, :, rows * per_chunk * u : rows * per_chunk * (u + 1)]
            term = jnp.dot(weights, rhs_ref[...], preferred_element_type=jnp.float32)
            acc = acc + term.astype(jnp.bfloat16).astype(jnp.float32)
        o_ref[:, lanes] = (q_ref[:, lanes].astype(jnp.float32) * acc).astype(o_ref.dtype)


def shards(queries, keys, values, taps, segment_ids):
    rows = queries.shape[0]
    channels = queries.shape[1]
    filters = taps.shape[1]
    group_size = channels // filters
    ctx_count = lax.axis_size("ctx")
    own_index = lax.axis_index("ctx")
    core = own_index % 2
    tap_rows = taps.shape[0]
    filt_len = tap_rows * ctx_count
    lags = filt_len // rows
    seg_row = jnp.zeros((1, filters), jnp.bfloat16).at[0, :rows].set(segment_ids.astype(jnp.bfloat16))
    packed = jnp.concatenate([taps, seg_row], axis=0)
    gated = (keys.astype(jnp.float32) * values.astype(jnp.float32)).astype(jnp.bfloat16)
    assert ctx_count & (ctx_count - 1) == 0
    steps = [ctx_count >> r for r in range(1, ctx_count.bit_length())]
    packed = gather_rounds(packed[None], "ctx", steps[:-1])
    packed, gated = lax.optimization_barrier((packed, gated))
    two_back = shifted(gated, "ctx", 2)
    four_back = shifted(gated, "ctx", 4)
    packed = unreversed(gather_rounds(packed, "ctx", steps[-1:]), ctx_count)
    all_taps = packed[:, :tap_rows].reshape(filt_len, filters).astype(jnp.float32)
    all_segs = packed[:, tap_rows, :rows].astype(jnp.int32)
    padded = jnp.concatenate(
        [
            jnp.zeros((filters, rows + 1), jnp.float32),
            all_taps.T[:, ::-1],
            jnp.zeros((filters, rows - 1), jnp.float32),
        ],
        axis=1,
    )
    seg_sources = [
        lax.dynamic_index_in_dim(all_segs, jnp.maximum(own_index - lag, 0), 0, keepdims=False)
        for lag in range(lags, -1, -1)
    ]
    mask = (segment_ids[:, None] == jnp.concatenate(seg_sources)[None, :]).astype(jnp.float32)
    lane_chunk = 128
    step_lanes = lane_chunk * 4 if channels % (lane_chunk * 4) == 0 else lane_chunk
    span = (lags + 1) * rows
    step_filters = step_lanes // group_size
    weights, own_term = pl.pallas_call(
        functools.partial(weight_kernel, lags=lags, rows=rows, group_size=group_size),
        grid=(channels // step_lanes,),
        in_specs=[
            pl.BlockSpec((step_filters, (lags + 2) * rows), lambda j: (j, 0)),
            pl.BlockSpec((rows, span), lambda j: (0, 0)),
            pl.BlockSpec((rows, step_lanes), lambda j: (0, j)),
        ],
        out_specs=[
            pl.BlockSpec((lags, rows, step_filters * rows), lambda j: (0, 0, j)),
            pl.BlockSpec((rows, step_lanes), lambda j: (0, j)),
        ],
        out_shape=[
            jax.ShapeDtypeStruct((lags, rows, filters * rows), jnp.bfloat16),
            jax.ShapeDtypeStruct((rows, channels), jnp.float32),
        ],
        scratch_shapes=[
            pltpu.VMEM((rows, rows * (lane_chunk // group_size)), jnp.bfloat16),
            pltpu.VMEM((rows * (lane_chunk // group_size), lane_chunk), jnp.bfloat16),
        ],
    )(padded, mask, gated)
    weights, own_term, four_back = lax.optimization_barrier((weights, own_term, four_back))
    swap_a = swapped(two_back, "ctx")
    own_out, _ = lax.optimization_barrier((gated, packed))
    pairs = [(source, source ^ 1) for source in range(ctx_count)]
    sibling_own = lax.ppermute(own_out, "ctx", [(s, d) for s, d in pairs if s % 2 == 0])
    sibling_four = lax.ppermute(four_back, "ctx", [(s, d) for s, d in pairs if s % 2 == 1])
    sources = [four_back, sibling_four, two_back, swap_a, sibling_own]
    kernel = functools.partial(conv_kernel, lags=lags, rows=rows, group_size=group_size)
    block = pl.BlockSpec((rows, step_lanes), lambda j, c: (0, j))
    return pl.pallas_call(
        kernel,
        grid_spec=pltpu.PrefetchScalarGridSpec(
            num_scalar_prefetch=1,
            grid=(channels // step_lanes,),
            in_specs=[block] * (lags + 1)
            + [
                pl.BlockSpec((lags, rows, step_filters * rows), lambda j, c: (0, 0, j)),
                block,
                block,
            ],
            out_specs=block,
            scratch_shapes=[pltpu.VMEM((rows * (lane_chunk // group_size), lane_chunk), jnp.bfloat16)],
        ),
        out_shape=jax.ShapeDtypeStruct((rows, channels), jnp.bfloat16),
    )(jnp.reshape(core, (1,)).astype(jnp.int32), *sources, weights, own_term, queries)


def solution(mesh):
    return jax.shard_map(
        shards,
        mesh=mesh,
        in_specs=(
            P(("dp", "ctx"), None),
            P(("dp", "ctx"), None),
            P(("dp", "ctx"), None),
            P("ctx", None),
            P(("dp", "ctx")),
        ),
        out_specs=P(("dp", "ctx"), None),
        check_vma=False,
    )
```
